256 devices in a mesh: row: 8 (over x_lo, y), col: 32 (over z, x_hi, core).
Axes of the slice: x: 4 (x_hi: 2, x_lo: 2; x = x_hi * 2 + x_lo), y: 4, z: 8, core: 2. Of those that a mesh axis runs over, the one named last changes fastest.
Arguments:
- frames: bfloat16 [1024, 8192], P('col', 'row'), may hold values from -6 to 6
- cotangent: bfloat16 [1024, 8192], P('col', 'row'), may hold values from -6 to 6
- gate_weight: bfloat16 [8192, 14336], P('row', 'col'), may hold values from -0.0625 to 0.0625
- up_weight: bfloat16 [8192, 14336], P('row', 'col'), may hold values from -0.0625 to 0.0625
- down_weight: bfloat16 [14336, 8192], P('col', 'row'), may hold values from -0.046875 to 0.046875
- utt_ids: int32 [1024], replicated, may hold values from 0 to 15, never falling along the last dimension, each value on 1 to 128 neighbouring positions
- valid_len: int32 [16], replicated, may hold values from 1 to 128
- time_start: int32 [16], replicated, may hold values from 0 to 127
- time_width: int32 [16], replicated, may hold values from 0 to 32
- freq_start: int32 [16], replicated, may hold values from 0 to 8191
- freq_width: int32 [16], replicated, may hold values from 0 to 2048
Outputs:
- output: bfloat16 [1024, 8192], P('col', 'row')
- grad_frames: bfloat16 [1024, 8192], P('col', 'row')
- grad_gate: bfloat16 [8192, 14336], P('row', 'col')
- grad_up: bfloat16 [8192, 14336], P('row', 'col')
- grad_down: bfloat16 [14336, 8192], P('col', 'row')
The draws below stay inside these ranges and needn't reach their ends.
Inputs may be any that keep to these rules, and one draw needn't show every extreme that they name: `utt_ids`: token ids never fall along the tokens; each utterance holds 1 to 128 tokens.
All inputs are finite; a program needn't handle non-finite values.
Results may differ from the reference program's by a relative error of at most 0.025.
Values may be sent and summed in bfloat16 or wider, within the bound.
No kernel may reach another device: no remote copies, remote signals or barrier semaphores. Data moves between devices by JAX's collectives and lax.ppermute only.
A program may use at most 64 MiB of HBM per device.

```python
import math
import jax
import jax.numpy as jnp
import numpy as np
from jax import lax

D = 8192
FF = 14336
UTTS = 16
TOKENS = 1024
MOSTLEN = 128
TIME_SPAN = 32
FREQ_SPAN = 2048
N_ROW = 8
N_COL = 32


def set_ends(values, key, least, largest):
    spot = [jax.random.randint(jax.random.fold_in(key, axis), (), 0, length) for axis, length in enumerate(values.shape)]
    main_axis = values.shape.index(max(values.shape))
    next_to = spot[:main_axis] + [(spot[main_axis] + 1) % values.shape[main_axis]] + spot[main_axis + 1:]
    return values.at[tuple(spot)].set(least).at[tuple(next_to)].set(largest)


def block_scale(own_key, extent, shards, smallest, top_value):
    factor_of = 1.0
    for axis_at, blocks in shards:
        heights = jax.random.uniform(jax.random.fold_in(jax.random.fold_in(own_key, 6), axis_at), (blocks,), jnp.float32, smallest / len(shards), top_value / len(shards))
        factor_of = factor_of * jnp.repeat(jnp.exp(heights), extent[axis_at] // blocks).reshape((-1,) + (1,) * (len(extent) - 1 - axis_at))
    return factor_of


def profile(number_of, total, limit, skew):
    weights = [(1 << 20) // math.isqrt(grade ** skew) + 1 for grade in range(2, number_of + 1)]
    spare, holding = total - limit - (number_of - 1), [1] * (number_of - 1)
    while spare > 0:
        candidates = [i for i in range(number_of - 1) if holding[i] < limit]
        whole, budget = sum([weights[i] for i in candidates]), spare
        for i in candidates:
            extra = min(limit - holding[i], max(1, budget * weights[i] // whole), spare)
            holding[i] = holding[i] + extra
            spare = spare - extra
    return np.array([limit] + holding)


def ragged(rng, number_of, total, limit, slope):
    if number_of == 2:
        one = jax.random.randint(rng, (), max(1, total - limit), min(limit, total - 1) + 1)
        return jnp.stack([one, total - one])
    lengths = jnp.asarray(profile(number_of, total, limit, slope), jnp.int32)
    couples = (number_of - 1) // 2
    donor, taker = lengths[1:1 + 2 * couples:2], lengths[2:2 + 2 * couples:2]
    room = jnp.minimum(donor - 1, limit - taker)
    moved = jax.random.randint(jax.random.fold_in(rng, 1), (couples,), 0, 1 << 20) % (room + 1)
    lengths = lengths.at[1:1 + 2 * couples:2].set(donor - moved).at[2:2 + 2 * couples:2].set(taker + moved)
    return lengths[jax.random.permutation(jax.random.fold_in(rng, 2), number_of)]


def scatter_about(own_key, dims, scale, most, cuts=(), kind=jnp.bfloat16):
    level = block_scale(own_key, dims, cuts, -0.22, 0.18) if cuts else 1.0
    entries = jax.random.normal(own_key, dims, jnp.float32) * scale * level
    return jnp.minimum(jnp.maximum(entries, -most), most).astype(kind)


def setup_inputs(seed: int = 0) -> dict:
    key_list = jax.random.split(jax.random.key(seed), 12)
    return {
        "frames": scatter_about(key_list[0], (TOKENS, D), 1.0, 6.0, ((0, 32), (1, 8))),
        "cotangent": scatter_about(key_list[1], (TOKENS, D), 1.0, 6.0, ((0, 32), (1, 8))),
        "gate_weight": scatter_about(key_list[2], (D, FF), D ** -0.5, 0.0625, ((0, 8), (1, 32))),
        "up_weight": scatter_about(key_list[3], (D, FF), D ** -0.5, 0.0625, ((0, 8), (1, 32))),
        "down_weight": scatter_about(key_list[4], (FF, D), FF ** -0.5, 0.046875, ((0, 32), (1, 8))),
        "utt_ids": jnp.searchsorted(jnp.cumsum(ragged(key_list[5], UTTS, TOKENS, MOSTLEN, 0)), jnp.arange(TOKENS), side="right").astype(jnp.int32),
        "valid_len": set_ends(jax.random.randint(key_list[6], (UTTS,), 1, MOSTLEN + 1), jax.random.fold_in(key_list[6], 1), 1, MOSTLEN).astype(jnp.int32),
        "time_start": set_ends(jax.random.randint(key_list[7], (UTTS,), 0, MOSTLEN), jax.random.fold_in(key_list[7], 1), 0, MOSTLEN - 1).astype(jnp.int32),
        "time_width": set_ends(jax.random.randint(key_list[8], (UTTS,), 0, TIME_SPAN + 1), jax.random.fold_in(key_list[8], 1), 0, TIME_SPAN).astype(jnp.int32),
        "freq_start": set_ends(jax.random.randint(key_list[9], (UTTS,), 0, D), jax.random.fold_in(key_list[9], 1), 0, D - 1).astype(jnp.int32),
        "freq_width": set_ends(jax.random.randint(key_list[10], (UTTS,), 0, FREQ_SPAN + 1), jax.random.fold_in(key_list[10], 1), 0, FREQ_SPAN).astype(jnp.int32),
    }


def span_masks(utt_ids, local_ids, tok_index, feat_index, valid_len, time_start, time_width, freq_start, freq_width):
    utt_index = jnp.arange(valid_len.shape[0], dtype=jnp.int32)
    starts = jnp.sum((utt_ids[None, :] < utt_index[:, None]).astype(jnp.int32), axis=1)
    member = (local_ids[:, None] == utt_index[None, :]).astype(jnp.int32)

    def lookup(table):
        return jnp.sum(member * table[None, :], axis=1)

    position = tok_index - lookup(starts)
    valid_rows = position < lookup(valid_len)
    time_low = lookup(time_start)
    in_time = (position >= time_low) & (position < time_low + lookup(time_width))
    freq_low = lookup(freq_start)[:, None]
    freq_high = freq_low + lookup(freq_width)[:, None]
    in_freq = (feat_index[None, :] >= freq_low) & (feat_index[None, :] < freq_high)
    keep_mask = (valid_rows & jnp.logical_not(in_time))[:, None] & jnp.logical_not(in_freq)
    return keep_mask, valid_rows


def rounded(value):
    return lax.optimization_barrier(value.astype(jnp.bfloat16)).astype(jnp.float32)


def blockwise(term, blocks, rows, cols):
    def step(index, total):
        return total + rounded(term(index))

    return lax.fori_loop(0, blocks, step, jnp.zeros((rows, cols), jnp.float32))


def reference(frames, cotangent, gate_weight, up_weight, down_weight, utt_ids, valid_len, time_start, time_width, freq_start, freq_width):
    total = frames.shape[0]
    width = frames.shape[1]
    hidden_units = gate_weight.shape[1]
    feat_block = width // N_ROW
    unit_block = hidden_units // N_COL
    tok_index = jnp.arange(total, dtype=jnp.int32)
    feat_index = jnp.arange(width, dtype=jnp.int32)
    keep_mask, valid_rows = span_masks(utt_ids, utt_ids, tok_index, feat_index, valid_len, time_start, time_width, freq_start, freq_width)
    masked = jnp.where(keep_mask, frames, jnp.zeros_like(frames))
    contract_last = (((1,), (1,)), ((), ()))
    contract_first = (((0,), (0,)), ((), ()))

    def feat_slice(array, index, axis):
        return lax.dynamic_slice_in_dim(array, (index * feat_block).astype(jnp.int32), feat_block, axis)

    def unit_slice(array, index, axis):
        return lax.dynamic_slice_in_dim(array, (index * unit_block).astype(jnp.int32), unit_block, axis)

    def gate_term(index):
        return jnp.dot(feat_slice(masked, index, 1), feat_slice(gate_weight, index, 0), preferred_element_type=jnp.float32)

    def up_term(index):
        return jnp.dot(feat_slice(masked, index, 1), feat_slice(up_weight, index, 0), preferred_element_type=jnp.float32)

    gate = blockwise(gate_term, N_ROW, total, hidden_units)
    up = blockwise(up_term, N_ROW, total, hidden_units)
    sigmoid_gate = jax.nn.sigmoid(gate)
    hidden = (gate * sigmoid_gate * up).astype(jnp.bfloat16)

    def output_term(index):
        return jnp.dot(unit_slice(hidden, index, 1), unit_slice(down_weight, index, 0), preferred_element_type=jnp.float32)

    output = blockwise(output_term, N_COL, total, width).astype(jnp.bfloat16)
    cot_valid = jnp.where(valid_rows[:, None], cotangent, jnp.zeros_like(cotangent))

    def hidden_grad_term(index):
        return lax.dot_general(feat_slice(cot_valid, index, 1), feat_slice(down_weight, index, 1), contract_last, preferred_element_type=jnp.float32)

    grad_hidden = blockwise(hidden_grad_term, N_ROW, total, hidden_units)
    dgate = (grad_hidden * up * sigmoid_gate * (1.0 + gate * (1.0 - sigmoid_gate))).astype(jnp.bfloat16)
    dup = (grad_hidden * gate * sigmoid_gate).astype(jnp.bfloat16)
    grad_down = lax.dot_general(hidden, cot_valid, contract_first, preferred_element_type=jnp.float32).astype(jnp.bfloat16)
    grad_gate = lax.dot_general(masked, dgate, contract_first, preferred_element_type=jnp.float32).astype(jnp.bfloat16)
    grad_up = lax.dot_general(masked, dup, contract_first, preferred_element_type=jnp.float32).astype(jnp.bfloat16)

    def input_grad_term(index):
        first = lax.dot_general(unit_slice(dgate, index, 1), unit_slice(gate_weight, index, 1), contract_last, preferred_element_type=jnp.float32)
        second = lax.dot_general(unit_slice(dup, index, 1), unit_slice(up_weight, index, 1), contract_last, preferred_element_type=jnp.float32)
        return first + second

    grad_masked = blockwise(input_grad_term, N_COL, total, width)
    grad_frames = jnp.where(keep_mask, grad_masked, jnp.zeros_like(grad_masked)).astype(jnp.bfloat16)
    return (output, grad_frames, grad_gate, grad_up, grad_down)
```

```python
import jax
import jax.numpy as jnp
from jax import lax
from jax.sharding import PartitionSpec as P


def span_masks(
    utt_ids,
    local_ids,
    tok_index,
    feat_index,
    valid_len,
    time_start,
    time_width,
    freq_start,
    freq_width,
):
    utt_index = jnp.arange(valid_len.shape[0], dtype=jnp.int32)
    starts = jnp.sum((utt_ids[None, :] < utt_index[:, None]).astype(jnp.int32), axis=1)
    member = (local_ids[:, None] == utt_index[None, :]).astype(jnp.int32)

    def lookup(table):
        return jnp.sum(member * table[None, :], axis=1)

    position = tok_index - lookup(starts)
    valid_rows = position < lookup(valid_len)
    time_low = lookup(time_start)
    in_time = (position >= time_low) & (position < time_low + lookup(time_width))
    freq_low = lookup(freq_start)[:, None]
    freq_high = freq_low + lookup(freq_width)[:, None]
    in_freq = (feat_index[None, :] >= freq_low) & (feat_index[None, :] < freq_high)
    keep_mask = (valid_rows & jnp.logical_not(in_time))[:, None] & jnp.logical_not(in_freq)
    return (keep_mask, valid_rows)


def shards(
    frames,
    cotangent,
    gate_weight,
    up_weight,
    down_weight,
    utt_ids,
    valid_len,
    time_start,
    time_width,
    freq_start,
    freq_width,
):
    tok_rows, feat_cols = frames.shape
    hidden_cols = gate_weight.shape[1]
    first_tok = lax.axis_index("col") * tok_rows
    first_feat = lax.axis_index("row") * feat_cols
    tok_index = first_tok + jnp.arange(tok_rows, dtype=jnp.int32)
    feat_index = first_feat + jnp.arange(feat_cols, dtype=jnp.int32)
    local_ids = lax.dynamic_slice_in_dim(utt_ids, first_tok, tok_rows)
    keep_mask, valid_rows = span_masks(
        utt_ids,
        local_ids,
        tok_index,
        feat_index,
        valid_len,
        time_start,
        time_width,
        freq_start,
        freq_width,
    )
    masked = jnp.where(keep_mask, frames, jnp.zeros_like(frames))
    cot_valid = jnp.where(valid_rows[:, None], cotangent, jnp.zeros_like(cotangent))
    contract_last = (((1,), (1,)), ((), ()))
    contract_first = (((0,), (0,)), ((), ()))
    both_all = lax.all_gather(
        jnp.concatenate([masked, cot_valid], axis=1), "col", axis=0, tiled=True
    )
    tokens_all = both_all[:, :feat_cols]
    cot_all = both_all[:, feat_cols:]
    sums = lax.psum_scatter(
        jnp.concatenate(
            [
                jnp.dot(tokens_all, gate_weight, preferred_element_type=jnp.float32),
                jnp.dot(tokens_all, up_weight, preferred_element_type=jnp.float32),
                lax.dot_general(
                    cot_all, down_weight, contract_last, preferred_element_type=jnp.float32
                ),
            ],
            axis=1,
        ).astype(jnp.bfloat16),
        "row",
        scatter_dimension=0,
        tiled=True,
    ).astype(jnp.float32)
    gate = sums[:, :hidden_cols]
    up = sums[:, hidden_cols : 2 * hidden_cols]
    grad_hidden = sums[:, 2 * hidden_cols :]
    sigmoid_gate = jax.nn.sigmoid(gate)
    hidden = (gate * sigmoid_gate * up).astype(jnp.bfloat16)
    dgate = (grad_hidden * up * sigmoid_gate * (1.0 + gate * (1.0 - sigmoid_gate))).astype(
        jnp.bfloat16
    )
    dup = (grad_hidden * gate * sigmoid_gate).astype(jnp.bfloat16)
    acts_all = lax.all_gather(
        jnp.concatenate([hidden, dgate, dup], axis=1), "row", axis=0, tiled=True
    )
    hidden_all = acts_all[:, :hidden_cols]
    dgate_all = acts_all[:, hidden_cols : 2 * hidden_cols]
    dup_all = acts_all[:, 2 * hidden_cols :]
    grad_down = lax.dot_general(
        hidden_all, cot_all, contract_first, preferred_element_type=jnp.float32
    ).astype(jnp.bfloat16)
    grad_gate = lax.dot_general(
        tokens_all, dgate_all, contract_first, preferred_element_type=jnp.float32
    ).astype(jnp.bfloat16)
    grad_up = lax.dot_general(
        tokens_all, dup_all, contract_first, preferred_element_type=jnp.float32
    ).astype(jnp.bfloat16)
    out_sums = lax.psum_scatter(
        jnp.concatenate(
            [
                jnp.dot(hidden_all, down_weight, preferred_element_type=jnp.float32).astype(
                    jnp.bfloat16
                ),
                (
                    lax.dot_general(
                        dgate_all, gate_weight, contract_last, preferred_element_type=jnp.float32
                    )
                    + lax.dot_general(
                        dup_all, up_weight, contract_last, preferred_element_type=jnp.float32
                    )
                ).astype(jnp.bfloat16),
            ],
            axis=1,
        ),
        "col",
        scatter_dimension=0,
        tiled=True,
    )
    output = out_sums[:, :feat_cols]
    grad_masked = out_sums[:, feat_cols:].astype(jnp.float32)
    grad_frames = jnp.where(keep_mask, grad_masked, jnp.zeros_like(grad_masked)).astype(
        jnp.bfloat16
    )
    return (output, grad_frames, grad_gate, grad_up, grad_down)


def solution(mesh):
    placed = (
        P("col", "row"),
        P("col", "row"),
        P("row", "col"),
        P("row", "col"),
        P("col", "row"),
        P(),
        P(),
        P(),
        P(),
        P(),
        P(),
    )
    return jax.shard_map(
        shards,
        mesh=mesh,
        in_specs=placed,
        out_specs=(
            P("col", "row"),
            P("col", "row"),
            P("row", "col"),
            P("row", "col"),
            P("col", "row"),
        ),
        check_vma=False,
    )
```

```python
import jax
import jax.numpy as jnp
from jax import lax
from jax.sharding import PartitionSpec as P


def span_masks(
    utt_ids,
    local_ids,
    tok_index,
    feat_index,
    valid_len,
    time_start,
    time_width,
    freq_start,
    freq_width,
):
    utt_index = jnp.arange(valid_len.shape[0], dtype=jnp.int32)
    starts = jnp.sum((utt_ids[None, :] < utt_index[:, None]).astype(jnp.int32), axis=1)
    member = (local_ids[:, None] == utt_index[None, :]).astype(jnp.int32)

    def lookup(table):
        return jnp.sum(member * table[None, :], axis=1)

    position = tok_index - lookup(starts)
    valid_rows = position < lookup(valid_len)
    time_low = lookup(time_start)
    in_time = (position >= time_low) & (position < time_low + lookup(time_width))
    freq_low = lookup(freq_start)[:, None]
    freq_high = freq_low + lookup(freq_width)[:, None]
    in_freq = (feat_index[None, :] >= freq_low) & (feat_index[None, :] < freq_high)
    keep_mask = (valid_rows & jnp.logical_not(in_time))[:, None] & jnp.logical_not(in_freq)
    return (keep_mask, valid_rows)


def gather_by_exchange(part, axis, count):
    spread = jnp.broadcast_to(part[None], (count,) + part.shape)
    got = lax.all_to_all(spread, axis, 0, 0)
    return got.reshape((count * part.shape[0],) + part.shape[1:])


def sum_by_exchange(partial, axis, count):
    split = partial.reshape((count, partial.shape[0] // count) + partial.shape[1:])
    got = lax.all_to_all(split, axis, 0, 0)
    return jnp.sum(got.astype(jnp.float32), axis=0)


def shards(
    frames,
    cotangent,
    gate_weight,
    up_weight,
    down_weight,
    utt_ids,
    valid_len,
    time_start,
    time_width,
    freq_start,
    freq_width,
):
    tok_rows, feat_cols = frames.shape
    hidden_cols = gate_weight.shape[1]
    first_tok = lax.axis_index("col") * tok_rows
    first_feat = lax.axis_index("row") * feat_cols
    tok_index = first_tok + jnp.arange(tok_rows, dtype=jnp.int32)
    feat_index = first_feat + jnp.arange(feat_cols, dtype=jnp.int32)
    local_ids = lax.dynamic_slice_in_dim(utt_ids, first_tok, tok_rows)
    keep_mask, valid_rows = span_masks(
        utt_ids,
        local_ids,
        tok_index,
        feat_index,
        valid_len,
        time_start,
        time_width,
        freq_start,
        freq_width,
    )
    masked = jnp.where(keep_mask, frames, jnp.zeros_like(frames))
    cot_valid = jnp.where(valid_rows[:, None], cotangent, jnp.zeros_like(cotangent))
    contract_last = (((1,), (1,)), ((), ()))
    contract_first = (((0,), (0,)), ((), ()))
    both_all = lax.all_gather(
        jnp.concatenate([masked, cot_valid], axis=1), "col", axis=0, tiled=True
    )
    tokens_all = both_all[:, :feat_cols]
    cot_all = both_all[:, feat_cols:]
    sums = sum_by_exchange(
        jnp.concatenate(
            [
                jnp.dot(tokens_all, gate_weight, preferred_element_type=jnp.float32),
                jnp.dot(tokens_all, up_weight, preferred_element_type=jnp.float32),
                lax.dot_general(
                    cot_all, down_weight, contract_last, preferred_element_type=jnp.float32
                ),
            ],
            axis=1,
        ).astype(jnp.bfloat16),
        "row",
        lax.psum(1, "row"),
    )
    gate = sums[:, :hidden_cols]
    up = sums[:, hidden_cols : 2 * hidden_cols]
    grad_hidden = sums[:, 2 * hidden_cols :]
    sigmoid_gate = jax.nn.sigmoid(gate)
    hidden = (gate * sigmoid_gate * up).astype(jnp.bfloat16)
    dgate = (grad_hidden * up * sigmoid_gate * (1.0 + gate * (1.0 - sigmoid_gate))).astype(
        jnp.bfloat16
    )
    dup = (grad_hidden * gate * sigmoid_gate).astype(jnp.bfloat16)
    acts_all = gather_by_exchange(
        jnp.concatenate([hidden, dgate, dup], axis=1), "row", lax.psum(1, "row")
    )
    hidden_all = acts_all[:, :hidden_cols]
    dgate_all = acts_all[:, hidden_cols : 2 * hidden_cols]
    dup_all = acts_all[:, 2 * hidden_cols :]
    grad_down = lax.dot_general(
        hidden_all, cot_all, contract_first, preferred_element_type=jnp.float32
    ).astype(jnp.bfloat16)
    grad_gate = lax.dot_general(
        tokens_all, dgate_all, contract_first, preferred_element_type=jnp.float32
    ).astype(jnp.bfloat16)
    grad_up = lax.dot_general(
        tokens_all, dup_all, contract_first, preferred_element_type=jnp.float32
    ).astype(jnp.bfloat16)
    out_sums = sum_by_exchange(
        jnp.concatenate(
            [
                jnp.dot(hidden_all, down_weight, preferred_element_type=jnp.float32).astype(
                    jnp.bfloat16
                ),
                (
                    lax.dot_general(
                        dgate_all, gate_weight, contract_last, preferred_element_type=jnp.float32
                    )
                    + lax.dot_general(
                        dup_all, up_weight, contract_last, preferred_element_type=jnp.float32
                    )
                ).astype(jnp.bfloat16),
            ],
            axis=1,
        ),
        "col",
        lax.psum(1, "col"),
    )
    output = out_sums[:, :feat_cols].astype(jnp.bfloat16)
    grad_masked = out_sums[:, feat_cols:]
    grad_frames = jnp.where(keep_mask, grad_masked, jnp.zeros_like(grad_masked)).astype(
        jnp.bfloat16
    )
    return (output, grad_frames, grad_gate, grad_up, grad_down)


def solution(mesh):
    placed = (
        P("col", "row"),
        P("col", "row"),
        P("row", "col"),
        P("row", "col"),
        P("col", "row"),
        P(),
        P(),
        P(),
        P(),
        P(),
        P(),
    )
    return jax.shard_map(
        shards,
        mesh=mesh,
        in_specs=placed,
        out_specs=(
            P("col", "row"),
            P("col", "row"),
            P("row", "col"),
            P("row", "col"),
            P("col", "row"),
        ),
        check_vma=False,
    )
```

```python
import jax
import jax.numpy as jnp
from jax import lax
from jax.sharding import Mesh, PartitionSpec as P

COL = ("cz", "cx", "cc")
CHIPS = ("cz", "cx")
CORE = "cc"


def span_masks(
    utt_ids,
    local_ids,
    tok_index,
    feat_index,
    valid_len,
    time_start,
    time_width,
    freq_start,
    freq_width,
):
    utt_index = jnp.arange(valid_len.shape[0], dtype=jnp.int32)
    starts = jnp.sum((utt_ids[None, :] < utt_index[:, None]).astype(jnp.int32), axis=1)
    member = (local_ids[:, None] == utt_index[None, :]).astype(jnp.int32)

    def lookup(table):
        return jnp.sum(member * table[None, :], axis=1)

    position = tok_index - lookup(starts)
    valid_rows = position < lookup(valid_len)
    time_low = lookup(time_start)
    in_time = (position >= time_low) & (position < time_low + lookup(time_width))
    freq_low = lookup(freq_start)[:, None]
    freq_high = freq_low + lookup(freq_width)[:, None]
    in_freq = (feat_index[None, :] >= freq_low) & (feat_index[None, :] < freq_high)
    keep_mask = (valid_rows & jnp.logical_not(in_time))[:, None] & jnp.logical_not(in_freq)
    return (keep_mask, valid_rows)


def gather_by_exchange(part, axis, count):
    spread = jnp.broadcast_to(part[None], (count,) + part.shape)
    got = lax.all_to_all(spread, axis, 0, 0)
    return got.reshape((count * part.shape[0],) + part.shape[1:])


def sum_by_exchange(partial, axis, count):
    split = partial.reshape((count, partial.shape[0] // count) + partial.shape[1:])
    got = lax.all_to_all(split, axis, 0, 0)
    return jnp.sum(got.astype(jnp.float32), axis=0)


def shards(
    frames,
    cotangent,
    gate_weight,
    up_weight,
    down_weight,
    utt_ids,
    valid_len,
    time_start,
    time_width,
    freq_start,
    freq_width,
):
    tok_rows, feat_cols = frames.shape
    hidden_cols = gate_weight.shape[1]
    first_tok = lax.axis_index(COL) * tok_rows
    first_feat = lax.axis_index("row") * feat_cols
    tok_index = first_tok + jnp.arange(tok_rows, dtype=jnp.int32)
    feat_index = first_feat + jnp.arange(feat_cols, dtype=jnp.int32)
    local_ids = lax.dynamic_slice_in_dim(utt_ids, first_tok, tok_rows)
    keep_mask, valid_rows = span_masks(
        utt_ids,
        local_ids,
        tok_index,
        feat_index,
        valid_len,
        time_start,
        time_width,
        freq_start,
        freq_width,
    )
    masked = jnp.where(keep_mask, frames, jnp.zeros_like(frames))
    cot_valid = jnp.where(valid_rows[:, None], cotangent, jnp.zeros_like(cotangent))
    contract_last = (((1,), (1,)), ((), ()))
    contract_first = (((0,), (0,)), ((), ()))
    both = jnp.concatenate([masked, cot_valid], axis=1)
    both_all = gather_by_exchange(
        gather_by_exchange(both, CHIPS, lax.psum(1, CHIPS)), CORE, lax.psum(1, CORE)
    )
    tokens_all = both_all[:, :feat_cols]
    cot_all = both_all[:, feat_cols:]
    sums = sum_by_exchange(
        jnp.concatenate(
            [
                jnp.dot(tokens_all, gate_weight, preferred_element_type=jnp.float32),
                jnp.dot(tokens_all, up_weight, preferred_element_type=jnp.float32),
                lax.dot_general(
                    cot_all, down_weight, contract_last, preferred_element_type=jnp.float32
                ),
            ],
            axis=1,
        ).astype(jnp.bfloat16),
        "row",
        lax.psum(1, "row"),
    )
    gate = sums[:, :hidden_cols]
    up = sums[:, hidden_cols : 2 * hidden_cols]
    grad_hidden = sums[:, 2 * hidden_cols :]
    sigmoid_gate = jax.nn.sigmoid(gate)
    hidden = (gate * sigmoid_gate * up).astype(jnp.bfloat16)
    dgate = (grad_hidden * up * sigmoid_gate * (1.0 + gate * (1.0 - sigmoid_gate))).astype(
        jnp.bfloat16
    )
    dup = (grad_hidden * gate * sigmoid_gate).astype(jnp.bfloat16)
    acts_all = gather_by_exchange(
        jnp.concatenate([hidden, dgate, dup], axis=1), "row", lax.psum(1, "row")
    )
    hidden_all = acts_all[:, :hidden_cols]
    dgate_all = acts_all[:, hidden_cols : 2 * hidden_cols]
    dup_all = acts_all[:, 2 * hidden_cols :]
    grad_down = lax.dot_general(
        hidden_all, cot_all, contract_first, preferred_element_type=jnp.float32
    ).astype(jnp.bfloat16)
    grad_gate = lax.dot_general(
        tokens_all, dgate_all, contract_first, preferred_element_type=jnp.float32
    ).astype(jnp.bfloat16)
    grad_up = lax.dot_general(
        tokens_all, dup_all, contract_first, preferred_element_type=jnp.float32
    ).astype(jnp.bfloat16)
    out_sums = sum_by_exchange(
        sum_by_exchange(
            jnp.concatenate(
            [
                jnp.dot(hidden_all, down_weight, preferred_element_type=jnp.float32).astype(
                    jnp.bfloat16
                ),
                (
                    lax.dot_general(
                        dgate_all, gate_weight, contract_last, preferred_element_type=jnp.float32
                    )
                    + lax.dot_general(
                        dup_all, up_weight, contract_last, preferred_element_type=jnp.float32
                    )
                ).astype(jnp.bfloat16),
            ],
            axis=1,
        ),
            CORE,
            lax.psum(1, CORE),
        ).astype(jnp.bfloat16),
        CHIPS,
        lax.psum(1, CHIPS),
    )
    output = out_sums[:, :feat_cols].astype(jnp.bfloat16)
    grad_masked = out_sums[:, feat_cols:]
    grad_frames = jnp.where(keep_mask, grad_masked, jnp.zeros_like(grad_masked)).astype(
        jnp.bfloat16
    )
    return (output, grad_frames, grad_gate, grad_up, grad_down)


def solution(mesh):
    n_row, n_col = mesh.devices.shape
    split = Mesh(mesh.devices.reshape(n_row, n_col // 4, 2, 2), ("row",) + COL)
    placed = (
        P(COL, "row"),
        P(COL, "row"),
        P("row", COL),
        P("row", COL),
        P(COL, "row"),
        P(),
        P(),
        P(),
        P(),
        P(),
        P(),
    )
    return jax.shard_map(
        shards,
        mesh=split,
        in_specs=placed,
        out_specs=(
            P(COL, "row"),
            P(COL, "row"),
            P("row", COL),
            P("row", COL),
            P(COL, "row"),
        ),
        check_vma=False,
    )
```

```python
import jax
import jax.numpy as jnp
from jax import lax
from jax.sharding import Mesh, PartitionSpec as P

COL = ("cz", "cx", "cc")
CHIPS = ("cz", "cx")
CORE = "cc"
LEVELS = ("cz", "cx", "cc")


def span_masks(
    utt_ids,
    local_ids,
    tok_index,
    feat_index,
    valid_len,
    time_start,
    time_width,
    freq_start,
    freq_width,
):
    utt_index = jnp.arange(valid_len.shape[0], dtype=jnp.int32)
    starts = jnp.sum((utt_ids[None, :] < utt_index[:, None]).astype(jnp.int32), axis=1)
    member = (local_ids[:, None] == utt_index[None, :]).astype(jnp.int32)

    def lookup(table):
        return jnp.sum(member * table[None, :], axis=1)

    position = tok_index - lookup(starts)
    valid_rows = position < lookup(valid_len)
    time_low = lookup(time_start)
    in_time = (position >= time_low) & (position < time_low + lookup(time_width))
    freq_low = lookup(freq_start)[:, None]
    freq_high = freq_low + lookup(freq_width)[:, None]
    in_freq = (feat_index[None, :] >= freq_low) & (feat_index[None, :] < freq_high)
    keep_mask = (valid_rows & jnp.logical_not(in_time))[:, None] & jnp.logical_not(in_freq)
    return (keep_mask, valid_rows)


def gather_by_exchange(part, axis, count):
    spread = jnp.broadcast_to(part[None], (count,) + part.shape)
    got = lax.all_to_all(spread, axis, 0, 0)
    return got.reshape((count * part.shape[0],) + part.shape[1:])


def sum_by_exchange(partial, axis, count):
    split = partial.reshape((count, partial.shape[0] // count) + partial.shape[1:])
    got = lax.all_to_all(split, axis, 0, 0)
    return jnp.sum(got.astype(jnp.float32), axis=0)


def shards(
    frames,
    cotangent,
    gate_weight,
    up_weight,
    down_weight,
    utt_ids,
    valid_len,
    time_start,
    time_width,
    freq_start,
    freq_width,
):
    tok_rows, feat_cols = frames.shape
    hidden_cols = gate_weight.shape[1]
    first_tok = lax.axis_index(COL) * tok_rows
    first_feat = lax.axis_index("row") * feat_cols
    tok_index = first_tok + jnp.arange(tok_rows, dtype=jnp.int32)
    feat_index = first_feat + jnp.arange(feat_cols, dtype=jnp.int32)
    local_ids = lax.dynamic_slice_in_dim(utt_ids, first_tok, tok_rows)
    keep_mask, valid_rows = span_masks(
        utt_ids,
        local_ids,
        tok_index,
        feat_index,
        valid_len,
        time_start,
        time_width,
        freq_start,
        freq_width,
    )
    masked = jnp.where(keep_mask, frames, jnp.zeros_like(frames))
    cot_valid = jnp.where(valid_rows[:, None], cotangent, jnp.zeros_like(cotangent))
    contract_last = (((1,), (1,)), ((), ()))
    contract_first = (((0,), (0,)), ((), ()))
    both_all = jnp.concatenate([masked, cot_valid], axis=1)
    for level in LEVELS:
        both_all = gather_by_exchange(both_all, level, lax.psum(1, level))
    tokens_all = both_all[:, :feat_cols]
    cot_all = both_all[:, feat_cols:]
    sums = sum_by_exchange(
        jnp.concatenate(
            [
                jnp.dot(tokens_all, gate_weight, preferred_element_type=jnp.float32),
                jnp.dot(tokens_all, up_weight, preferred_element_type=jnp.float32),
                lax.dot_general(
                    cot_all, down_weight, contract_last, preferred_element_type=jnp.float32
                ),
            ],
            axis=1,
        ).astype(jnp.bfloat16),
        "row",
        lax.psum(1, "row"),
    )
    gate = sums[:, :hidden_cols]
    up = sums[:, hidden_cols : 2 * hidden_cols]
    grad_hidden = sums[:, 2 * hidden_cols :]
    sigmoid_gate = jax.nn.sigmoid(gate)
    hidden = (gate * sigmoid_gate * up).astype(jnp.bfloat16)
    dgate = (grad_hidden * up * sigmoid_gate * (1.0 + gate * (1.0 - sigmoid_gate))).astype(
        jnp.bfloat16
    )
    dup = (grad_hidden * gate * sigmoid_gate).astype(jnp.bfloat16)
    acts_all = gather_by_exchange(
        jnp.concatenate([hidden, dgate, dup], axis=1), "row", lax.psum(1, "row")
    )
    hidden_all = acts_all[:, :hidden_cols]
    dgate_all = acts_all[:, hidden_cols : 2 * hidden_cols]
    dup_all = acts_all[:, 2 * hidden_cols :]
    grad_down = lax.dot_general(
        hidden_all, cot_all, contract_first, preferred_element_type=jnp.float32
    ).astype(jnp.bfloat16)
    grad_gate = lax.dot_general(
        tokens_all, dgate_all, contract_first, preferred_element_type=jnp.float32
    ).astype(jnp.bfloat16)
    grad_up = lax.dot_general(
        tokens_all, dup_all, contract_first, preferred_element_type=jnp.float32
    ).astype(jnp.bfloat16)
    out_sums = jnp.concatenate(
        [
            jnp.dot(hidden_all, down_weight, preferred_element_type=jnp.float32).astype(
                jnp.bfloat16
            ),
            (
                lax.dot_general(
                    dgate_all, gate_weight, contract_last, preferred_element_type=jnp.float32
                )
                + lax.dot_general(
                    dup_all, up_weight, contract_last, preferred_element_type=jnp.float32
                )
            ).astype(jnp.bfloat16),
        ],
        axis=1,
    )
    for level in reversed(LEVELS):
        if level != LEVELS[-1]:
            out_sums = out_sums.astype(jnp.bfloat16)
        out_sums = sum_by_exchange(out_sums, level, lax.psum(1, level))
    output = out_sums[:, :feat_cols].astype(jnp.bfloat16)
    grad_masked = out_sums[:, feat_cols:]
    grad_frames = jnp.where(keep_mask, grad_masked, jnp.zeros_like(grad_masked)).astype(
        jnp.bfloat16
    )
    return (output, grad_frames, grad_gate, grad_up, grad_down)


def solution(mesh):
    n_row, n_col = mesh.devices.shape
    split = Mesh(mesh.devices.reshape(n_row, n_col // 4, 2, 2), ("row",) + COL)
    placed = (
        P(COL, "row"),
        P(COL, "row"),
        P("row", COL),
        P("row", COL),
        P(COL, "row"),
        P(),
        P(),
        P(),
        P(),
        P(),
        P(),
    )
    return jax.shard_map(
        shards,
        mesh=split,
        in_specs=placed,
        out_specs=(
            P(COL, "row"),
            P(COL, "row"),
            P("row", COL),
            P("row", COL),
            P(COL, "row"),
        ),
        check_vma=False,
    )
```

```python
import jax
import jax.numpy as jnp
from jax import lax
from jax.sharding import Mesh, PartitionSpec as P

COL = ("cz", "cx", "cc")
CHIPS = ("cz", "cx")
CORE = "cc"


def span_masks(
    utt_ids,
    local_ids,
    tok_index,
    feat_index,
    valid_len,
    time_start,
    time_width,
    freq_start,
    freq_width,
):
    utt_index = jnp.arange(valid_len.shape[0], dtype=jnp.int32)
    starts = jnp.sum((utt_ids[None, :] < utt_index[:, None]).astype(jnp.int32), axis=1)
    member = (local_ids[:, None] == utt_index[None, :]).astype(jnp.int32)

    def lookup(table):
        return jnp.sum(member * table[None, :], axis=1)

    position = tok_index - lookup(starts)
    valid_rows = position < lookup(valid_len)
    time_low = lookup(time_start)
    in_time = (position >= time_low) & (position < time_low + lookup(time_width))
    freq_low = lookup(freq_start)[:, None]
    freq_high = freq_low + lookup(freq_width)[:, None]
    in_freq = (feat_index[None, :] >= freq_low) & (feat_index[None, :] < freq_high)
    keep_mask = (valid_rows & jnp.logical_not(in_time))[:, None] & jnp.logical_not(in_freq)
    return (keep_mask, valid_rows)


def gather_by_exchange(part, axis, count):
    spread = jnp.broadcast_to(part[None], (count,) + part.shape)
    got = lax.all_to_all(spread, axis, 0, 0)
    return got.reshape((count * part.shape[0],) + part.shape[1:])


def sum_by_exchange(partial, axis, count):
    split = partial.reshape((count, partial.shape[0] // count) + partial.shape[1:])
    got = lax.all_to_all(split, axis, 0, 0).astype(jnp.float32)
    total = got[0]
    for index in range(1, count):
        total = total + got[index]
    return total


def shards(
    frames,
    cotangent,
    gate_weight,
    up_weight,
    down_weight,
    utt_ids,
    valid_len,
    time_start,
    time_width,
    freq_start,
    freq_width,
):
    tok_rows, feat_cols = frames.shape
    hidden_cols = gate_weight.shape[1]
    first_tok = lax.axis_index(COL) * tok_rows
    first_feat = lax.axis_index("row") * feat_cols
    tok_index = first_tok + jnp.arange(tok_rows, dtype=jnp.int32)
    feat_index = first_feat + jnp.arange(feat_cols, dtype=jnp.int32)
    local_ids = lax.dynamic_slice_in_dim(utt_ids, first_tok, tok_rows)
    keep_mask, valid_rows = span_masks(
        utt_ids,
        local_ids,
        tok_index,
        feat_index,
        valid_len,
        time_start,
        time_width,
        freq_start,
        freq_width,
    )
    masked = jnp.where(keep_mask, frames, jnp.zeros_like(frames))
    cot_valid = jnp.where(valid_rows[:, None], cotangent, jnp.zeros_like(cotangent))
    contract_last = (((1,), (1,)), ((), ()))
    contract_first = (((0,), (0,)), ((), ()))
    both = jnp.concatenate([masked, cot_valid], axis=1)
    both_all = gather_by_exchange(
        gather_by_exchange(both, CHIPS, lax.psum(1, CHIPS)), CORE, lax.psum(1, CORE)
    )
    tokens_all = both_all[:, :feat_cols]
    cot_all = both_all[:, feat_cols:]
    sums = sum_by_exchange(
        jnp.concatenate(
            [
                jnp.dot(tokens_all, gate_weight, preferred_element_type=jnp.float32),
                jnp.dot(tokens_all, up_weight, preferred_element_type=jnp.float32),
                lax.dot_general(
                    cot_all, down_weight, contract_last, preferred_element_type=jnp.float32
                ),
            ],
            axis=1,
        ).astype(jnp.bfloat16),
        "row",
        lax.psum(1, "row"),
    )
    gate = sums[:, :hidden_cols]
    up = sums[:, hidden_cols : 2 * hidden_cols]
    grad_hidden = sums[:, 2 * hidden_cols :]
    sigmoid_gate = jax.nn.sigmoid(gate)
    hidden = (gate * sigmoid_gate * up).astype(jnp.bfloat16)
    dgate = (grad_hidden * up * sigmoid_gate * (1.0 + gate * (1.0 - sigmoid_gate))).astype(
        jnp.bfloat16
    )
    dup = (grad_hidden * gate * sigmoid_gate).astype(jnp.bfloat16)
    acts_all = gather_by_exchange(
        jnp.concatenate([hidden, dgate, dup], axis=1), "row", lax.psum(1, "row")
    )
    hidden_all = acts_all[:, :hidden_cols]
    dgate_all = acts_all[:, hidden_cols : 2 * hidden_cols]
    dup_all = acts_all[:, 2 * hidden_cols :]
    grad_down = lax.dot_general(
        hidden_all, cot_all, contract_first, preferred_element_type=jnp.float32
    ).astype(jnp.bfloat16)
    grad_gate = lax.dot_general(
        tokens_all, dgate_all, contract_first, preferred_element_type=jnp.float32
    ).astype(jnp.bfloat16)
    grad_up = lax.dot_general(
        tokens_all, dup_all, contract_first, preferred_element_type=jnp.float32
    ).astype(jnp.bfloat16)
    out_sums = sum_by_exchange(
        sum_by_exchange(
            jnp.concatenate(
            [
                jnp.dot(hidden_all, down_weight, preferred_element_type=jnp.float32).astype(
                    jnp.bfloat16
                ),
                (
                    lax.dot_general(
                        dgate_all, gate_weight, contract_last, preferred_element_type=jnp.float32
                    )
                    + lax.dot_general(
                        dup_all, up_weight, contract_last, preferred_element_type=jnp.float32
                    )
                ).astype(jnp.bfloat16),
            ],
            axis=1,
        ),
            CORE,
            lax.psum(1, CORE),
        ).astype(jnp.bfloat16),
        CHIPS,
        lax.psum(1, CHIPS),
    )
    output = out_sums[:, :feat_cols].astype(jnp.bfloat16)
    grad_masked = out_sums[:, feat_cols:]
    grad_frames = jnp.where(keep_mask, grad_masked, jnp.zeros_like(grad_masked)).astype(
        jnp.bfloat16
    )
    return (output, grad_frames, grad_gate, grad_up, grad_down)


def solution(mesh):
    n_row, n_col = mesh.devices.shape
    split = Mesh(mesh.devices.reshape(n_row, n_col // 4, 2, 2), ("row",) + COL)
    placed = (
        P(COL, "row"),
        P(COL, "row"),
        P("row", COL),
        P("row", COL),
        P(COL, "row"),
        P(),
        P(),
        P(),
        P(),
        P(),
        P(),
    )
    return jax.shard_map(
        shards,
        mesh=split,
        in_specs=placed,
        out_specs=(
            P(COL, "row"),
            P(COL, "row"),
            P("row", COL),
            P("row", COL),
            P(COL, "row"),
        ),
        check_vma=False,
    )
```

```python
import jax
import jax.numpy as jnp
from jax import lax
from jax.sharding import Mesh, PartitionSpec as P

COL = ("cz", "cx", "cc")
CHIPS = ("cz", "cx")
CORE = "cc"


def span_masks(
    utt_ids,
    local_ids,
    tok_index,
    feat_index,
    valid_len,
    time_start,
    time_width,
    freq_start,
    freq_width,
):
    utt_index = jnp.arange(valid_len.shape[0], dtype=jnp.int32)
    starts = jnp.sum((utt_ids[None, :] < utt_index[:, None]).astype(jnp.int32), axis=1)
    member = (local_ids[:, None] == utt_index[None, :]).astype(jnp.int32)

    def lookup(table):
        return jnp.sum(member * table[None, :], axis=1)

    position = tok_index - lookup(starts)
    valid_rows = position < lookup(valid_len)
    time_low = lookup(time_start)
    in_time = (position >= time_low) & (position < time_low + lookup(time_width))
    freq_low = lookup(freq_start)[:, None]
    freq_high = freq_low + lookup(freq_width)[:, None]
    in_freq = (feat_index[None, :] >= freq_low) & (feat_index[None, :] < freq_high)
    keep_mask = (valid_rows & jnp.logical_not(in_time))[:, None] & jnp.logical_not(in_freq)
    return (keep_mask, valid_rows)


def gather_by_exchange(part, axis, count):
    spread = jnp.broadcast_to(part[None], (count,) + part.shape)
    got = lax.all_to_all(spread, axis, 0, 0)
    return got.reshape((count * part.shape[0],) + part.shape[1:])


def sum_by_exchange(partial, axis, count):
    split = partial.reshape((count, partial.shape[0] // count) + partial.shape[1:])
    got = lax.all_to_all(split, axis, 0, 0)
    return jnp.sum(got.astype(jnp.float32), axis=0)


def shards(
    frames,
    cotangent,
    gate_weight,
    up_weight,
    down_weight,
    utt_ids,
    valid_len,
    time_start,
    time_width,
    freq_start,
    freq_width,
):
    tok_rows, feat_cols = frames.shape
    hidden_cols = gate_weight.shape[1]
    first_tok = lax.axis_index(COL) * tok_rows
    first_feat = lax.axis_index("row") * feat_cols
    tok_index = first_tok + jnp.arange(tok_rows, dtype=jnp.int32)
    feat_index = first_feat + jnp.arange(feat_cols, dtype=jnp.int32)
    local_ids = lax.dynamic_slice_in_dim(utt_ids, first_tok, tok_rows)
    keep_mask, valid_rows = span_masks(
        utt_ids,
        local_ids,
        tok_index,
        feat_index,
        valid_len,
        time_start,
        time_width,
        freq_start,
        freq_width,
    )
    contract_last = (((1,), (1,)), ((), ()))
    contract_first = (((0,), (0,)), ((), ()))
    n_chips, n_core = lax.psum(1, CHIPS), lax.psum(1, CORE)
    raw_all = gather_by_exchange(
        gather_by_exchange(jnp.concatenate([frames, cotangent], axis=1), CHIPS, n_chips),
        CORE,
        n_core,
    )
    spot = jnp.arange(raw_all.shape[0], dtype=jnp.int32)
    chunk = n_chips * tok_rows
    all_index = ((spot % chunk) // tok_rows * n_core + spot // chunk) * tok_rows + spot % tok_rows
    keep_all, valid_all = span_masks(
        utt_ids,
        jnp.take(utt_ids, all_index),
        all_index,
        feat_index,
        valid_len,
        time_start,
        time_width,
        freq_start,
        freq_width,
    )
    both_all = jnp.concatenate(
        [
            jnp.where(keep_all, raw_all[:, :feat_cols], jnp.zeros_like(raw_all[:, :feat_cols])),
            jnp.where(
                valid_all[:, None], raw_all[:, feat_cols:], jnp.zeros_like(raw_all[:, feat_cols:])
            ),
        ],
        axis=1,
    )
    tokens_all = both_all[:, :feat_cols]
    cot_all = both_all[:, feat_cols:]
    sums = sum_by_exchange(
        jnp.concatenate(
            [
                jnp.dot(tokens_all, gate_weight, preferred_element_type=jnp.float32),
                jnp.dot(tokens_all, up_weight, preferred_element_type=jnp.float32),
                lax.dot_general(
                    cot_all, down_weight, contract_last, preferred_element_type=jnp.float32
                ),
            ],
            axis=1,
        ).astype(jnp.bfloat16),
        "row",
        lax.psum(1, "row"),
    )
    gate = sums[:, :hidden_cols]
    up = sums[:, hidden_cols : 2 * hidden_cols]
    grad_hidden = sums[:, 2 * hidden_cols :]
    sigmoid_gate = jax.nn.sigmoid(gate)
    hidden = (gate * sigmoid_gate * up).astype(jnp.bfloat16)
    dgate = (grad_hidden * up * sigmoid_gate * (1.0 + gate * (1.0 - sigmoid_gate))).astype(
        jnp.bfloat16
    )
    dup = (grad_hidden * gate * sigmoid_gate).astype(jnp.bfloat16)
    acts_all = gather_by_exchange(
        jnp.concatenate([hidden, dgate, dup], axis=1), "row", lax.psum(1, "row")
    )
    hidden_all = acts_all[:, :hidden_cols]
    dgate_all = acts_all[:, hidden_cols : 2 * hidden_cols]
    dup_all = acts_all[:, 2 * hidden_cols :]
    grad_down = lax.dot_general(
        hidden_all, cot_all, contract_first, preferred_element_type=jnp.float32
    ).astype(jnp.bfloat16)
    grad_gate = lax.dot_general(
        tokens_all, dgate_all, contract_first, preferred_element_type=jnp.float32
    ).astype(jnp.bfloat16)
    grad_up = lax.dot_general(
        tokens_all, dup_all, contract_first, preferred_element_type=jnp.float32
    ).astype(jnp.bfloat16)
    out_sums = sum_by_exchange(
        sum_by_exchange(
            jnp.concatenate(
            [
                jnp.dot(hidden_all, down_weight, preferred_element_type=jnp.float32).astype(
                    jnp.bfloat16
                ),
                (
                    lax.dot_general(
                        dgate_all, gate_weight, contract_last, preferred_element_type=jnp.float32
                    )
                    + lax.dot_general(
                        dup_all, up_weight, contract_last, preferred_element_type=jnp.float32
                    )
                ).astype(jnp.bfloat16),
            ],
            axis=1,
        ),
            CORE,
            lax.psum(1, CORE),
        ).astype(jnp.bfloat16),
        CHIPS,
        lax.psum(1, CHIPS),
    )
    output = out_sums[:, :feat_cols].astype(jnp.bfloat16)
    grad_masked = out_sums[:, feat_cols:]
    grad_frames = jnp.where(keep_mask, grad_masked, jnp.zeros_like(grad_masked)).astype(
        jnp.bfloat16
    )
    return (output, grad_frames, grad_gate, grad_up, grad_down)


def solution(mesh):
    n_row, n_col = mesh.devices.shape
    split = Mesh(mesh.devices.reshape(n_row, n_col // 4, 2, 2), ("row",) + COL)
    placed = (
        P(COL, "row"),
        P(COL, "row"),
        P("row", COL),
        P("row", COL),
        P(COL, "row"),
        P(),
        P(),
        P(),
        P(),
        P(),
        P(),
    )
    return jax.shard_map(
        shards,
        mesh=split,
        in_specs=placed,
        out_specs=(
            P(COL, "row"),
            P(COL, "row"),
            P("row", COL),
            P("row", COL),
            P(COL, "row"),
        ),
        check_vma=False,
    )
```

```python
import jax
import jax.numpy as jnp
from jax import lax
from jax.experimental.layout import Layout, with_layout_constraint
from jax.sharding import Mesh, PartitionSpec as P

COL = ("cz", "cx", "cc")
CHIPS = ("cz", "cx")
CORE = "cc"


def span_masks(
    utt_ids,
    local_ids,
    tok_index,
    feat_index,
    valid_len,
    time_start,
    time_width,
    freq_start,
    freq_width,
):
    utt_index = jnp.arange(valid_len.shape[0], dtype=jnp.int32)
    starts = jnp.sum((utt_ids[None, :] < utt_index[:, None]).astype(jnp.int32), axis=1)
    member = (local_ids[:, None] == utt_index[None, :]).astype(jnp.int32)

    def lookup(table):
        return jnp.sum(member * table[None, :], axis=1)

    position = tok_index - lookup(starts)
    valid_rows = position < lookup(valid_len)
    time_low = lookup(time_start)
    in_time = (position >= time_low) & (position < time_low + lookup(time_width))
    freq_low = lookup(freq_start)[:, None]
    freq_high = freq_low + lookup(freq_width)[:, None]
    in_freq = (feat_index[None, :] >= freq_low) & (feat_index[None, :] < freq_high)
    keep_mask = (valid_rows & jnp.logical_not(in_time))[:, None] & jnp.logical_not(in_freq)
    return (keep_mask, valid_rows)


def tokens_major(value):
    return with_layout_constraint(value, Layout((0, 1)))


def gather_by_exchange(part, axis, count):
    spread = jnp.broadcast_to(part[None], (count,) + part.shape)
    got = lax.all_to_all(spread, axis, 0, 0)
    return got.reshape((count * part.shape[0],) + part.shape[1:])


def sum_by_exchange(partial, axis, count):
    split = partial.reshape((count, partial.shape[0] // count) + partial.shape[1:])
    got = lax.all_to_all(split, axis, 0, 0)
    return jnp.sum(got.astype(jnp.float32), axis=0)


def shards(
    frames,
    cotangent,
    gate_weight,
    up_weight,
    down_weight,
    utt_ids,
    valid_len,
    time_start,
    time_width,
    freq_start,
    freq_width,
):
    tok_rows, feat_cols = frames.shape
    hidden_cols = gate_weight.shape[1]
    first_tok = lax.axis_index(COL) * tok_rows
    first_feat = lax.axis_index("row") * feat_cols
    tok_index = first_tok + jnp.arange(tok_rows, dtype=jnp.int32)
    feat_index = first_feat + jnp.arange(feat_cols, dtype=jnp.int32)
    local_ids = lax.dynamic_slice_in_dim(utt_ids, first_tok, tok_rows)
    keep_mask, valid_rows = span_masks(
        utt_ids,
        local_ids,
        tok_index,
        feat_index,
        valid_len,
        time_start,
        time_width,
        freq_start,
        freq_width,
    )
    masked = jnp.where(keep_mask, frames, jnp.zeros_like(frames))
    cot_valid = jnp.where(valid_rows[:, None], cotangent, jnp.zeros_like(cotangent))
    contract_last = (((1,), (1,)), ((), ()))
    contract_first = (((0,), (0,)), ((), ()))
    both = jnp.concatenate([masked, cot_valid], axis=1)
    both_all = gather_by_exchange(
        gather_by_exchange(both, CHIPS, lax.psum(1, CHIPS)), CORE, lax.psum(1, CORE)
    )
    tokens_all = both_all[:, :feat_cols]
    cot_all = both_all[:, feat_cols:]
    sums = sum_by_exchange(
        jnp.concatenate(
            [
                jnp.dot(tokens_all, gate_weight, preferred_element_type=jnp.float32),
                jnp.dot(tokens_all, up_weight, preferred_element_type=jnp.float32),
                lax.dot_general(
                    cot_all, down_weight, contract_last, preferred_element_type=jnp.float32
                ),
            ],
            axis=1,
        ).astype(jnp.bfloat16),
        "row",
        lax.psum(1, "row"),
    )
    gate = sums[:, :hidden_cols]
    up = sums[:, hidden_cols : 2 * hidden_cols]
    grad_hidden = sums[:, 2 * hidden_cols :]
    sigmoid_gate = jax.nn.sigmoid(gate)
    hidden = (gate * sigmoid_gate * up).astype(jnp.bfloat16)
    dgate = (grad_hidden * up * sigmoid_gate * (1.0 + gate * (1.0 - sigmoid_gate))).astype(
        jnp.bfloat16
    )
    dup = (grad_hidden * gate * sigmoid_gate).astype(jnp.bfloat16)
    acts_all = gather_by_exchange(
        jnp.concatenate([hidden, dgate, dup], axis=1), "row", lax.psum(1, "row")
    )
    hidden_all = acts_all[:, :hidden_cols]
    dgate_all = acts_all[:, hidden_cols : 2 * hidden_cols]
    dup_all = acts_all[:, 2 * hidden_cols :]
    grad_down = lax.dot_general(
        hidden_all, cot_all, contract_first, preferred_element_type=jnp.float32
    ).astype(jnp.bfloat16)
    grad_gate = lax.dot_general(
        tokens_all, dgate_all, contract_first, preferred_element_type=jnp.float32
    ).astype(jnp.bfloat16)
    grad_up = lax.dot_general(
        tokens_all, dup_all, contract_first, preferred_element_type=jnp.float32
    ).astype(jnp.bfloat16)
    out_sums = sum_by_exchange(
        sum_by_exchange(
            tokens_major(jnp.concatenate(
            [
                jnp.dot(hidden_all, down_weight, preferred_element_type=jnp.float32).astype(
                    jnp.bfloat16
                ),
                (
                    lax.dot_general(
                        dgate_all, gate_weight, contract_last, preferred_element_type=jnp.float32
                    )
                    + lax.dot_general(
                        dup_all, up_weight, contract_last, preferred_element_type=jnp.float32
                    )
                ).astype(jnp.bfloat16),
            ],
            axis=1,
        )),
            CORE,
            lax.psum(1, CORE),
        ).astype(jnp.bfloat16),
        CHIPS,
        lax.psum(1, CHIPS),
    )
    output = out_sums[:, :feat_cols].astype(jnp.bfloat16)
    grad_masked = out_sums[:, feat_cols:]
    grad_frames = jnp.where(keep_mask, grad_masked, jnp.zeros_like(grad_masked)).astype(
        jnp.bfloat16
    )
    return (output, grad_frames, grad_gate, grad_up, grad_down)


def solution(mesh):
    n_row, n_col = mesh.devices.shape
    split = Mesh(mesh.devices.reshape(n_row, n_col // 4, 2, 2), ("row",) + COL)
    placed = (
        P(COL, "row"),
        P(COL, "row"),
        P("row", COL),
        P("row", COL),
        P(COL, "row"),
        P(),
        P(),
        P(),
        P(),
        P(),
        P(),
    )
    return jax.shard_map(
        shards,
        mesh=split,
        in_specs=placed,
        out_specs=(
            P(COL, "row"),
            P(COL, "row"),
            P("row", COL),
            P("row", COL),
            P(COL, "row"),
        ),
        check_vma=False,
    )
```

```python
import jax
import jax.numpy as jnp
from jax import lax
from jax.experimental.layout import Layout, with_layout_constraint
from jax.sharding import Mesh, PartitionSpec as P

COL = ("cz", "cx", "cc")
CHIPS = ("cz", "cx")
CORE = "cc"


def span_masks(
    utt_ids,
    local_ids,
    tok_index,
    feat_index,
    valid_len,
    time_start,
    time_width,
    freq_start,
    freq_width,
):
    utt_index = jnp.arange(valid_len.shape[0], dtype=jnp.int32)
    starts = jnp.sum((utt_ids[None, :] < utt_index[:, None]).astype(jnp.int32), axis=1)
    member = (local_ids[:, None] == utt_index[None, :]).astype(jnp.int32)

    def lookup(table):
        return jnp.sum(member * table[None, :], axis=1)

    position = tok_index - lookup(starts)
    valid_rows = position < lookup(valid_len)
    time_low = lookup(time_start)
    in_time = (position >= time_low) & (position < time_low + lookup(time_width))
    freq_low = lookup(freq_start)[:, None]
    freq_high = freq_low + lookup(freq_width)[:, None]
    in_freq = (feat_index[None, :] >= freq_low) & (feat_index[None, :] < freq_high)
    keep_mask = (valid_rows & jnp.logical_not(in_time))[:, None] & jnp.logical_not(in_freq)
    return (keep_mask, valid_rows)


def tokens_major(value):
    return with_layout_constraint(value, Layout((0, 1)))


def gather_by_exchange(part, axis, count):
    spread = jnp.broadcast_to(part[None], (count,) + part.shape)
    got = lax.all_to_all(spread, axis, 0, 0)
    return got.reshape((count * part.shape[0],) + part.shape[1:])


def sum_by_exchange(partial, axis, count):
    split = partial.reshape((count, partial.shape[0] // count) + partial.shape[1:])
    got = lax.all_to_all(split, axis, 0, 0)
    if count > 2:
        return jnp.sum(got.astype(jnp.float32), axis=0)
    return got[0].astype(jnp.float32) + got[1].astype(jnp.float32)


def shards(
    frames,
    cotangent,
    gate_weight,
    up_weight,
    down_weight,
    utt_ids,
    valid_len,
    time_start,
    time_width,
    freq_start,
    freq_width,
):
    tok_rows, feat_cols = frames.shape
    hidden_cols = gate_weight.shape[1]
    first_tok = lax.axis_index(COL) * tok_rows
    first_feat = lax.axis_index("row") * feat_cols
    tok_index = first_tok + jnp.arange(tok_rows, dtype=jnp.int32)
    feat_index = first_feat + jnp.arange(feat_cols, dtype=jnp.int32)
    local_ids = lax.dynamic_slice_in_dim(utt_ids, first_tok, tok_rows)
    keep_mask, valid_rows = span_masks(
        utt_ids,
        local_ids,
        tok_index,
        feat_index,
        valid_len,
        time_start,
        time_width,
        freq_start,
        freq_width,
    )
    masked = jnp.where(keep_mask, frames, jnp.zeros_like(frames))
    cot_valid = jnp.where(valid_rows[:, None], cotangent, jnp.zeros_like(cotangent))
    contract_last = (((1,), (1,)), ((), ()))
    contract_first = (((0,), (0,)), ((), ()))
    both = jnp.concatenate([masked, cot_valid], axis=1)
    both_all = gather_by_exchange(
        gather_by_exchange(both, CHIPS, lax.psum(1, CHIPS)), CORE, lax.psum(1, CORE)
    )
    tokens_all = both_all[:, :feat_cols]
    cot_all = both_all[:, feat_cols:]
    sums = sum_by_exchange(
        jnp.concatenate(
            [
                jnp.dot(tokens_all, gate_weight, preferred_element_type=jnp.float32),
                jnp.dot(tokens_all, up_weight, preferred_element_type=jnp.float32),
                lax.dot_general(
                    cot_all, down_weight, contract_last, preferred_element_type=jnp.float32
                ),
            ],
            axis=1,
        ).astype(jnp.bfloat16),
        "row",
        lax.psum(1, "row"),
    )
    gate = sums[:, :hidden_cols]
    up = sums[:, hidden_cols : 2 * hidden_cols]
    grad_hidden = sums[:, 2 * hidden_cols :]
    sigmoid_gate = jax.nn.sigmoid(gate)
    hidden = (gate * sigmoid_gate * up).astype(jnp.bfloat16)
    dgate = (grad_hidden * up * sigmoid_gate * (1.0 + gate * (1.0 - sigmoid_gate))).astype(
        jnp.bfloat16
    )
    dup = (grad_hidden * gate * sigmoid_gate).astype(jnp.bfloat16)
    acts_all = gather_by_exchange(
        jnp.concatenate([hidden, dgate, dup], axis=1), "row", lax.psum(1, "row")
    )
    hidden_all = acts_all[:, :hidden_cols]
    dgate_all = acts_all[:, hidden_cols : 2 * hidden_cols]
    dup_all = acts_all[:, 2 * hidden_cols :]
    grad_down = lax.dot_general(
        hidden_all, cot_all, contract_first, preferred_element_type=jnp.float32
    ).astype(jnp.bfloat16)
    grad_gate = lax.dot_general(
        tokens_all, dgate_all, contract_first, preferred_element_type=jnp.float32
    ).astype(jnp.bfloat16)
    grad_up = lax.dot_general(
        tokens_all, dup_all, contract_first, preferred_element_type=jnp.float32
    ).astype(jnp.bfloat16)
    out_sums = sum_by_exchange(
        sum_by_exchange(
            tokens_major(jnp.concatenate(
            [
                jnp.dot(hidden_all, down_weight, preferred_element_type=jnp.float32).astype(
                    jnp.bfloat16
                ),
                (
                    lax.dot_general(
                        dgate_all, gate_weight, contract_last, preferred_element_type=jnp.float32
                    )
                    + lax.dot_general(
                        dup_all, up_weight, contract_last, preferred_element_type=jnp.float32
                    )
                ).astype(jnp.bfloat16),
            ],
            axis=1,
        )),
            CORE,
            lax.psum(1, CORE),
        ).astype(jnp.bfloat16),
        CHIPS,
        lax.psum(1, CHIPS),
    )
    output = out_sums[:, :feat_cols].astype(jnp.bfloat16)
    grad_masked = out_sums[:, feat_cols:]
    grad_frames = jnp.where(keep_mask, grad_masked, jnp.zeros_like(grad_masked)).astype(
        jnp.bfloat16
    )
    return (output, grad_frames, grad_gate, grad_up, grad_down)


def solution(mesh):
    n_row, n_col = mesh.devices.shape
    split = Mesh(mesh.devices.reshape(n_row, n_col // 4, 2, 2), ("row",) + COL)
    placed = (
        P(COL, "row"),
        P(COL, "row"),
        P("row", COL),
        P("row", COL),
        P(COL, "row"),
        P(),
        P(),
        P(),
        P(),
        P(),
        P(),
    )
    return jax.shard_map(
        shards,
        mesh=split,
        in_specs=placed,
        out_specs=(
            P(COL, "row"),
            P(COL, "row"),
            P("row", COL),
            P("row", COL),
            P(COL, "row"),
        ),
        check_vma=False,
    )
```

```python
import jax
import jax.numpy as jnp
from jax import lax
from jax.experimental.layout import Layout, with_layout_constraint
from jax.sharding import Mesh, PartitionSpec as P

COL = ("cz", "cx", "cc")
CHIPS = ("cz", "cx")
CORE = "cc"


def span_masks(
    utt_ids,
    local_ids,
    tok_index,
    feat_index,
    valid_len,
    time_start,
    time_width,
    freq_start,
    freq_width,
):
    utt_index = jnp.arange(valid_len.shape[0], dtype=jnp.int32)
    starts = jnp.sum((utt_ids[None, :] < utt_index[:, None]).astype(jnp.int32), axis=1)
    member = (local_ids[:, None] == utt_index[None, :]).astype(jnp.int32)

    def lookup(table):
        return jnp.sum(member * table[None, :], axis=1)

    position = tok_index - lookup(starts)
    valid_rows = position < lookup(valid_len)
    time_low = lookup(time_start)
    in_time = (position >= time_low) & (position < time_low + lookup(time_width))
    freq_low = lookup(freq_start)[:, None]
    freq_high = freq_low + lookup(freq_width)[:, None]
    in_freq = (feat_index[None, :] >= freq_low) & (feat_index[None, :] < freq_high)
    keep_mask = (valid_rows & jnp.logical_not(in_time))[:, None] & jnp.logical_not(in_freq)
    return (keep_mask, valid_rows)


def tokens_major(value):
    return with_layout_constraint(value, Layout((0, 1)))


def gather_by_exchange(part, axis, count):
    spread = jnp.broadcast_to(part[None], (count,) + part.shape)
    got = lax.all_to_all(spread, axis, 0, 0)
    return got.reshape((count * part.shape[0],) + part.shape[1:])


def sum_by_exchange(partial, axis, count):
    split = partial.reshape((count, partial.shape[0] // count) + partial.shape[1:])
    got = lax.all_to_all(split, axis, 0, 0)
    if count > 2:
        return jnp.sum(got.astype(jnp.float32), axis=0)
    return got[0].astype(jnp.float32) + got[1].astype(jnp.float32)


def shards(
    frames,
    cotangent,
    gate_weight,
    up_weight,
    down_weight,
    utt_ids,
    valid_len,
    time_start,
    time_width,
    freq_start,
    freq_width,
):
    tok_rows, feat_cols = frames.shape
    hidden_cols = gate_weight.shape[1]
    first_tok = lax.axis_index(COL) * tok_rows
    first_feat = lax.axis_index("row") * feat_cols
    tok_index = first_tok + jnp.arange(tok_rows, dtype=jnp.int32)
    feat_index = first_feat + jnp.arange(feat_cols, dtype=jnp.int32)
    local_ids = lax.dynamic_slice_in_dim(utt_ids, first_tok, tok_rows)
    keep_mask, valid_rows = span_masks(
        utt_ids,
        local_ids,
        tok_index,
        feat_index,
        valid_len,
        time_start,
        time_width,
        freq_start,
        freq_width,
    )
    masked = jnp.where(keep_mask, frames, jnp.zeros_like(frames))
    cot_valid = jnp.where(valid_rows[:, None], cotangent, jnp.zeros_like(cotangent))
    contract_last = (((1,), (1,)), ((), ()))
    contract_first = (((0,), (0,)), ((), ()))
    both = jnp.concatenate([masked, cot_valid], axis=1)
    both_all = gather_by_exchange(
        gather_by_exchange(both, CHIPS, lax.psum(1, CHIPS)), CORE, lax.psum(1, CORE)
    )
    tokens_all = both_all[:, :feat_cols]
    cot_all = both_all[:, feat_cols:]
    sums = sum_by_exchange(
        jnp.concatenate(
            [
                jnp.dot(tokens_all, gate_weight, preferred_element_type=jnp.float32),
                jnp.dot(tokens_all, up_weight, preferred_element_type=jnp.float32),
                lax.dot_general(
                    cot_all, down_weight, contract_last, preferred_element_type=jnp.float32
                ),
            ],
            axis=1,
        ).astype(jnp.bfloat16),
        "row",
        lax.psum(1, "row"),
    )
    gate = sums[:, :hidden_cols]
    up = sums[:, hidden_cols : 2 * hidden_cols]
    grad_hidden = sums[:, 2 * hidden_cols :]
    sigmoid_gate = jax.nn.sigmoid(gate)
    hidden = (gate * sigmoid_gate * up).astype(jnp.bfloat16)
    dgate = (grad_hidden * up * sigmoid_gate * (1.0 + gate * (1.0 - sigmoid_gate))).astype(
        jnp.bfloat16
    )
    dup = (grad_hidden * gate * sigmoid_gate).astype(jnp.bfloat16)
    acts_all = gather_by_exchange(
        jnp.concatenate([hidden, dgate, dup], axis=1), "row", lax.psum(1, "row")
    )
    hidden_all = acts_all[:, :hidden_cols]
    dgate_all = acts_all[:, hidden_cols : 2 * hidden_cols]
    dup_all = acts_all[:, 2 * hidden_cols :]
    grad_down = lax.dot_general(
        hidden_all, cot_all, contract_first, preferred_element_type=jnp.float32
    ).astype(jnp.bfloat16)
    grad_gate = lax.dot_general(
        tokens_all, dgate_all, contract_first, preferred_element_type=jnp.float32
    ).astype(jnp.bfloat16)
    grad_up = lax.dot_general(
        tokens_all, dup_all, contract_first, preferred_element_type=jnp.float32
    ).astype(jnp.bfloat16)
    out_partial = jnp.concatenate(
        [
            jnp.dot(hidden_all, down_weight, preferred_element_type=jnp.float32).astype(
                jnp.bfloat16
            ),
            (
                lax.dot_general(
                    dgate_all, gate_weight, contract_last, preferred_element_type=jnp.float32
                )
                + lax.dot_general(
                    dup_all, up_weight, contract_last, preferred_element_type=jnp.float32
                )
            ).astype(jnp.bfloat16),
        ],
        axis=1,
    )
    chip_sums = sum_by_exchange(tokens_major(out_partial), CORE, lax.psum(1, CORE))
    out_sums = sum_by_exchange(chip_sums.astype(jnp.bfloat16), CHIPS, lax.psum(1, CHIPS))
    output = out_sums[:, :feat_cols].astype(jnp.bfloat16)
    grad_masked = out_sums[:, feat_cols:]
    grad_frames = jnp.where(keep_mask, grad_masked, jnp.zeros_like(grad_masked)).astype(
        jnp.bfloat16
    )
    return (output, grad_frames, grad_gate, grad_up, grad_down)


def solution(mesh):
    n_row, n_col = mesh.devices.shape
    split = Mesh(mesh.devices.reshape(n_row, n_col // 4, 2, 2), ("row",) + COL)
    placed = (
        P(COL, "row"),
        P(COL, "row"),
        P("row", COL),
        P("row", COL),
        P(COL, "row"),
        P(),
        P(),
        P(),
        P(),
        P(),
        P(),
    )
    return jax.shard_map(
        shards,
        mesh=split,
        in_specs=placed,
        out_specs=(
            P(COL, "row"),
            P(COL, "row"),
            P("row", COL),
            P("row", COL),
            P(COL, "row"),
        ),
        check_vma=False,
    )
```

```python
import jax
import jax.numpy as jnp
from jax import lax
from jax.experimental.layout import Layout, with_layout_constraint
from jax.sharding import Mesh, PartitionSpec as P

COL = ("cz", "cx", "cc")
CHIPS = ("cz", "cx")
CORE = "cc"


def span_masks(
    utt_ids,
    tok_index,
    feat_index,
    valid_len,
    time_start,
    time_width,
    freq_start,
    freq_width,
):
    utt_index = jnp.arange(valid_len.shape[0], dtype=jnp.int32)
    starts = jnp.sum((utt_ids[None, :] < utt_index[:, None]).astype(jnp.int32), axis=1)
    ends = jnp.sum((utt_ids[None, :] <= utt_index[:, None]).astype(jnp.int32), axis=1)
    member = (
        (tok_index[:, None] >= starts[None, :]) & (tok_index[:, None] < ends[None, :])
    ).astype(jnp.int32)

    def lookup(table):
        return jnp.sum(member * table[None, :], axis=1)

    position = tok_index - lookup(starts)
    valid_rows = position < lookup(valid_len)
    time_low = lookup(time_start)
    in_time = (position >= time_low) & (position < time_low + lookup(time_width))
    freq_low = lookup(freq_start)[:, None]
    freq_high = freq_low + lookup(freq_width)[:, None]
    in_freq = (feat_index[None, :] >= freq_low) & (feat_index[None, :] < freq_high)
    keep_mask = (valid_rows & jnp.logical_not(in_time))[:, None] & jnp.logical_not(in_freq)
    return (keep_mask, valid_rows)


def tokens_major(value):
    return with_layout_constraint(value, Layout((0, 1)))


def gather_by_exchange(part, axis, count):
    spread = jnp.broadcast_to(part[None], (count,) + part.shape)
    got = lax.all_to_all(spread, axis, 0, 0)
    return got.reshape((count * part.shape[0],) + part.shape[1:])


def sum_by_exchange(partial, axis, count):
    split = partial.reshape((count, partial.shape[0] // count) + partial.shape[1:])
    got = lax.all_to_all(split, axis, 0, 0)
    if count > 2:
        return jnp.sum(got.astype(jnp.float32), axis=0)
    return got[0].astype(jnp.float32) + got[1].astype(jnp.float32)


def shards(
    frames,
    cotangent,
    gate_weight,
    up_weight,
    down_weight,
    utt_ids,
    valid_len,
    time_start,
    time_width,
    freq_start,
    freq_width,
):
    tok_rows, feat_cols = frames.shape
    hidden_cols = gate_weight.shape[1]
    first_tok = lax.axis_index(COL) * tok_rows
    first_feat = lax.axis_index("row") * feat_cols
    tok_index = first_tok + jnp.arange(tok_rows, dtype=jnp.int32)
    feat_index = first_feat + jnp.arange(feat_cols, dtype=jnp.int32)
    keep_mask, valid_rows = span_masks(
        utt_ids,
        tok_index,
        feat_index,
        valid_len,
        time_start,
        time_width,
        freq_start,
        freq_width,
    )
    masked = jnp.where(keep_mask, frames, jnp.zeros_like(frames))
    cot_valid = jnp.where(valid_rows[:, None], cotangent, jnp.zeros_like(cotangent))
    contract_last = (((1,), (1,)), ((), ()))
    contract_first = (((0,), (0,)), ((), ()))
    both = jnp.concatenate([masked, cot_valid], axis=1)
    both_all = gather_by_exchange(
        gather_by_exchange(both, CHIPS, lax.psum(1, CHIPS)), CORE, lax.psum(1, CORE)
    )
    tokens_all = both_all[:, :feat_cols]
    cot_all = both_all[:, feat_cols:]
    sums = sum_by_exchange(
        jnp.concatenate(
            [
                jnp.dot(tokens_all, gate_weight, preferred_element_type=jnp.float32),
                jnp.dot(tokens_all, up_weight, preferred_element_type=jnp.float32),
                lax.dot_general(
                    cot_all, down_weight, contract_last, preferred_element_type=jnp.float32
                ),
            ],
            axis=1,
        ).astype(jnp.bfloat16),
        "row",
        lax.psum(1, "row"),
    )
    gate = sums[:, :hidden_cols]
    up = sums[:, hidden_cols : 2 * hidden_cols]
    grad_hidden = sums[:, 2 * hidden_cols :]
    sigmoid_gate = jax.nn.sigmoid(gate)
    hidden = (gate * sigmoid_gate * up).astype(jnp.bfloat16)
    dgate = (grad_hidden * up * sigmoid_gate * (1.0 + gate * (1.0 - sigmoid_gate))).astype(
        jnp.bfloat16
    )
    dup = (grad_hidden * gate * sigmoid_gate).astype(jnp.bfloat16)
    acts_all = gather_by_exchange(
        jnp.concatenate([hidden, dgate, dup], axis=1), "row", lax.psum(1, "row")
    )
    hidden_all = acts_all[:, :hidden_cols]
    dgate_all = acts_all[:, hidden_cols : 2 * hidden_cols]
    dup_all = acts_all[:, 2 * hidden_cols :]
    grad_down = lax.dot_general(
        hidden_all, cot_all, contract_first, preferred_element_type=jnp.float32
    ).astype(jnp.bfloat16)
    grad_gate = lax.dot_general(
        tokens_all, dgate_all, contract_first, preferred_element_type=jnp.float32
    ).astype(jnp.bfloat16)
    grad_up = lax.dot_general(
        tokens_all, dup_all, contract_first, preferred_element_type=jnp.float32
    ).astype(jnp.bfloat16)
    out_partial = jnp.concatenate(
        [
            jnp.dot(hidden_all, down_weight, preferred_element_type=jnp.float32).astype(
                jnp.bfloat16
            ),
            (
                lax.dot_general(
                    dgate_all, gate_weight, contract_last, preferred_element_type=jnp.float32
                )
                + lax.dot_general(
                    dup_all, up_weight, contract_last, preferred_element_type=jnp.float32
                )
            ).astype(jnp.bfloat16),
        ],
        axis=1,
    )
    chip_sums = sum_by_exchange(tokens_major(out_partial), CORE, lax.psum(1, CORE))
    out_sums = sum_by_exchange(chip_sums.astype(jnp.bfloat16), CHIPS, lax.psum(1, CHIPS))
    output = out_sums[:, :feat_cols].astype(jnp.bfloat16)
    grad_masked = out_sums[:, feat_cols:]
    grad_frames = jnp.where(keep_mask, grad_masked, jnp.zeros_like(grad_masked)).astype(
        jnp.bfloat16
    )
    return (output, grad_frames, grad_gate, grad_up, grad_down)


def solution(mesh):
    n_row, n_col = mesh.devices.shape
    split = Mesh(mesh.devices.reshape(n_row, n_col // 4, 2, 2), ("row",) + COL)
    placed = (
        P(COL, "row"),
        P(COL, "row"),
        P("row", COL),
        P("row", COL),
        P(COL, "row"),
        P(),
        P(),
        P(),
        P(),
        P(),
        P(),
    )
    return jax.shard_map(
        shards,
        mesh=split,
        in_specs=placed,
        out_specs=(
            P(COL, "row"),
            P(COL, "row"),
            P("row", COL),
            P("row", COL),
            P(COL, "row"),
        ),
        check_vma=False,
    )
```

```python
import jax
import jax.numpy as jnp
from jax import lax
from jax.experimental.layout import Layout, with_layout_constraint
from jax.sharding import Mesh, PartitionSpec as P

COL = ("cz", "cx", "cc")
CHIPS = ("cz", "cx")
CORE = "cc"


def span_masks(
    utt_ids,
    tok_index,
    feat_index,
    valid_len,
    time_start,
    time_width,
    freq_start,
    freq_width,
):
    utt_index = jnp.arange(valid_len.shape[0], dtype=jnp.int32)
    starts = jnp.sum((utt_ids[None, :] < utt_index[:, None]).astype(jnp.int32), axis=1)
    ends = jnp.sum((utt_ids[None, :] <= utt_index[:, None]).astype(jnp.int32), axis=1)
    member = (
        (tok_index[:, None] >= starts[None, :]) & (tok_index[:, None] < ends[None, :])
    ).astype(jnp.int32)

    def lookup(table):
        return jnp.sum(member * table[None, :], axis=1)

    position = tok_index - lookup(starts)
    valid_rows = position < lookup(valid_len)
    time_low = lookup(time_start)
    in_time = (position >= time_low) & (position < time_low + lookup(time_width))
    freq_low = lookup(freq_start)[:, None]
    freq_high = freq_low + lookup(freq_width)[:, None]
    in_freq = (feat_index[None, :] >= freq_low) & (feat_index[None, :] < freq_high)
    keep_mask = (valid_rows & jnp.logical_not(in_time))[:, None] & jnp.logical_not(in_freq)
    return (keep_mask, valid_rows)


def tokens_major(value):
    return with_layout_constraint(value, Layout((0, 1)))


def swap_cores(value):
    return lax.ppermute(value, CORE, [(0, 1), (1, 0)])


def gather_by_exchange(part, axis, count):
    spread = jnp.broadcast_to(part[None], (count,) + part.shape)
    got = lax.all_to_all(spread, axis, 0, 0)
    return got.reshape((count * part.shape[0],) + part.shape[1:])


def sum_by_exchange(partial, axis, count):
    split = partial.reshape((count, partial.shape[0] // count) + partial.shape[1:])
    got = lax.all_to_all(split, axis, 0, 0)
    if count > 2:
        return jnp.sum(got.astype(jnp.float32), axis=0)
    return got[0].astype(jnp.float32) + got[1].astype(jnp.float32)


def shards(
    frames,
    cotangent,
    gate_weight,
    up_weight,
    down_weight,
    utt_ids,
    valid_len,
    time_start,
    time_width,
    freq_start,
    freq_width,
):
    tok_rows, feat_cols = frames.shape
    hidden_cols = gate_weight.shape[1]
    first_tok = lax.axis_index(COL) * tok_rows
    first_feat = lax.axis_index("row") * feat_cols
    tok_index = first_tok + jnp.arange(tok_rows, dtype=jnp.int32)
    feat_index = first_feat + jnp.arange(feat_cols, dtype=jnp.int32)
    keep_mask, valid_rows = span_masks(
        utt_ids,
        tok_index,
        feat_index,
        valid_len,
        time_start,
        time_width,
        freq_start,
        freq_width,
    )
    masked = jnp.where(keep_mask, frames, jnp.zeros_like(frames))
    cot_valid = jnp.where(valid_rows[:, None], cotangent, jnp.zeros_like(cotangent))
    contract_last = (((1,), (1,)), ((), ()))
    contract_first = (((0,), (0,)), ((), ()))
    both = jnp.concatenate([masked, cot_valid], axis=1)
    both_own = gather_by_exchange(both, CHIPS, lax.psum(1, CHIPS))
    both_all = jnp.concatenate([both_own, swap_cores(both_own)], axis=0)
    tokens_all = both_all[:, :feat_cols]
    cot_all = both_all[:, feat_cols:]
    sums = sum_by_exchange(
        jnp.concatenate(
            [
                jnp.dot(tokens_all, gate_weight, preferred_element_type=jnp.float32),
                jnp.dot(tokens_all, up_weight, preferred_element_type=jnp.float32),
                lax.dot_general(
                    cot_all, down_weight, contract_last, preferred_element_type=jnp.float32
                ),
            ],
            axis=1,
        ).astype(jnp.bfloat16),
        "row",
        lax.psum(1, "row"),
    )
    gate = sums[:, :hidden_cols]
    up = sums[:, hidden_cols : 2 * hidden_cols]
    grad_hidden = sums[:, 2 * hidden_cols :]
    sigmoid_gate = jax.nn.sigmoid(gate)
    hidden = (gate * sigmoid_gate * up).astype(jnp.bfloat16)
    dgate = (grad_hidden * up * sigmoid_gate * (1.0 + gate * (1.0 - sigmoid_gate))).astype(
        jnp.bfloat16
    )
    dup = (grad_hidden * gate * sigmoid_gate).astype(jnp.bfloat16)
    acts_all = gather_by_exchange(
        jnp.concatenate([hidden, dgate, dup], axis=1), "row", lax.psum(1, "row")
    )
    hidden_all = acts_all[:, :hidden_cols]
    dgate_all = acts_all[:, hidden_cols : 2 * hidden_cols]
    dup_all = acts_all[:, 2 * hidden_cols :]
    grad_down = lax.dot_general(
        hidden_all, cot_all, contract_first, preferred_element_type=jnp.float32
    ).astype(jnp.bfloat16)
    grad_gate = lax.dot_general(
        tokens_all, dgate_all, contract_first, preferred_element_type=jnp.float32
    ).astype(jnp.bfloat16)
    grad_up = lax.dot_general(
        tokens_all, dup_all, contract_first, preferred_element_type=jnp.float32
    ).astype(jnp.bfloat16)
    out_partial = jnp.concatenate(
        [
            jnp.dot(hidden_all, down_weight, preferred_element_type=jnp.float32).astype(
                jnp.bfloat16
            ),
            (
                lax.dot_general(
                    dgate_all, gate_weight, contract_last, preferred_element_type=jnp.float32
                )
                + lax.dot_general(
                    dup_all, up_weight, contract_last, preferred_element_type=jnp.float32
                )
            ).astype(jnp.bfloat16),
        ],
        axis=1,
    )
    out_partial = tokens_major(out_partial)
    half = out_partial.shape[0] // 2
    chip_sums = out_partial[:half].astype(jnp.float32) + swap_cores(out_partial[half:]).astype(
        jnp.float32
    )
    out_sums = sum_by_exchange(chip_sums.astype(jnp.bfloat16), CHIPS, lax.psum(1, CHIPS))
    output = out_sums[:, :feat_cols].astype(jnp.bfloat16)
    grad_masked = out_sums[:, feat_cols:]
    grad_frames = jnp.where(keep_mask, grad_masked, jnp.zeros_like(grad_masked)).astype(
        jnp.bfloat16
    )
    return (output, grad_frames, grad_gate, grad_up, grad_down)


def solution(mesh):
    n_row, n_col = mesh.devices.shape
    split = Mesh(mesh.devices.reshape(n_row, n_col // 4, 2, 2), ("row",) + COL)
    placed = (
        P(COL, "row"),
        P(COL, "row"),
        P("row", COL),
        P("row", COL),
        P(COL, "row"),
        P(),
        P(),
        P(),
        P(),
        P(),
        P(),
    )
    return jax.shard_map(
        shards,
        mesh=split,
        in_specs=placed,
        out_specs=(
            P(COL, "row"),
            P(COL, "row"),
            P("row", COL),
            P("row", COL),
            P(COL, "row"),
        ),
        check_vma=False,
    )
```

```python
import jax
import jax.numpy as jnp
from jax import lax
from jax.experimental.layout import Layout, with_layout_constraint
from jax.sharding import Mesh, PartitionSpec as P

COL = ("cz", "cx", "cc")
CHIPS = ("cz", "cx")
CORE = "cc"


def span_masks(
    utt_ids,
    tok_index,
    feat_index,
    valid_len,
    time_start,
    time_width,
    freq_start,
    freq_width,
):
    utt_index = jnp.arange(valid_len.shape[0], dtype=jnp.int32)
    starts = jnp.sum((utt_ids[None, :] < utt_index[:, None]).astype(jnp.int32), axis=1)
    ends = jnp.sum((utt_ids[None, :] <= utt_index[:, None]).astype(jnp.int32), axis=1)
    member = (
        (tok_index[:, None] >= starts[None, :]) & (tok_index[:, None] < ends[None, :])
    ).astype(jnp.int32)

    def lookup(table):
        return jnp.sum(member * table[None, :], axis=1)

    position = tok_index - lookup(starts)
    valid_rows = position < lookup(valid_len)
    time_low = lookup(time_start)
    in_time = (position >= time_low) & (position < time_low + lookup(time_width))
    freq_low = lookup(freq_start)[:, None]
    freq_high = freq_low + lookup(freq_width)[:, None]
    in_freq = (feat_index[None, :] >= freq_low) & (feat_index[None, :] < freq_high)
    keep_mask = (valid_rows & jnp.logical_not(in_time))[:, None] & jnp.logical_not(in_freq)
    return (keep_mask, valid_rows)


def tokens_major(value):
    return with_layout_constraint(value, Layout((0, 1)))


def swap_cores(value):
    return lax.ppermute(value, CORE, [(0, 1), (1, 0)])


def gather_by_exchange(part, axis, count):
    spread = jnp.broadcast_to(part[None], (count,) + part.shape)
    got = lax.all_to_all(spread, axis, 0, 0)
    return got.reshape((count * part.shape[0],) + part.shape[1:])


def sum_by_exchange(partial, axis, count):
    split = partial.reshape((count, partial.shape[0] // count) + partial.shape[1:])
    got = lax.all_to_all(split, axis, 0, 0)
    if count > 2:
        return jnp.sum(got.astype(jnp.float32), axis=0)
    return got[0].astype(jnp.float32) + got[1].astype(jnp.float32)


def shards(
    frames,
    cotangent,
    gate_weight,
    up_weight,
    down_weight,
    utt_ids,
    valid_len,
    time_start,
    time_width,
    freq_start,
    freq_width,
):
    tok_rows, feat_cols = frames.shape
    hidden_cols = gate_weight.shape[1]
    first_tok = lax.axis_index(COL) * tok_rows
    first_feat = lax.axis_index("row") * feat_cols
    tok_index = first_tok + jnp.arange(tok_rows, dtype=jnp.int32)
    feat_index = first_feat + jnp.arange(feat_cols, dtype=jnp.int32)
    keep_mask, valid_rows = span_masks(
        utt_ids,
        tok_index,
        feat_index,
        valid_len,
        time_start,
        time_width,
        freq_start,
        freq_width,
    )
    masked = jnp.where(keep_mask, frames, jnp.zeros_like(frames))
    cot_valid = jnp.where(valid_rows[:, None], cotangent, jnp.zeros_like(cotangent))
    contract_last = (((1,), (1,)), ((), ()))
    contract_first = (((0,), (0,)), ((), ()))
    both = jnp.concatenate([masked, cot_valid], axis=1)
    both_own = gather_by_exchange(both, CHIPS, lax.psum(1, CHIPS))
    both_other = swap_cores(both_own)
    both_all = jnp.concatenate([both_own, both_other], axis=0)
    tokens_all = both_all[:, :feat_cols]
    cot_all = both_all[:, feat_cols:]

    def row_partial(rows):
        return jnp.concatenate(
            [
                jnp.dot(rows[:, :feat_cols], gate_weight, preferred_element_type=jnp.float32),
                jnp.dot(rows[:, :feat_cols], up_weight, preferred_element_type=jnp.float32),
                lax.dot_general(
                    rows[:, feat_cols:], down_weight, contract_last, preferred_element_type=jnp.float32
                ),
            ],
            axis=1,
        ).astype(jnp.bfloat16)

    sums = sum_by_exchange(
        jnp.concatenate([row_partial(both_own), row_partial(both_other)], axis=0),
        "row",
        lax.psum(1, "row"),
    )
    gate = sums[:, :hidden_cols]
    up = sums[:, hidden_cols : 2 * hidden_cols]
    grad_hidden = sums[:, 2 * hidden_cols :]
    sigmoid_gate = jax.nn.sigmoid(gate)
    hidden = (gate * sigmoid_gate * up).astype(jnp.bfloat16)
    dgate = (grad_hidden * up * sigmoid_gate * (1.0 + gate * (1.0 - sigmoid_gate))).astype(
        jnp.bfloat16
    )
    dup = (grad_hidden * gate * sigmoid_gate).astype(jnp.bfloat16)
    acts_all = gather_by_exchange(
        jnp.concatenate([hidden, dgate, dup], axis=1), "row", lax.psum(1, "row")
    )
    hidden_all = acts_all[:, :hidden_cols]
    dgate_all = acts_all[:, hidden_cols : 2 * hidden_cols]
    dup_all = acts_all[:, 2 * hidden_cols :]
    grad_down = lax.dot_general(
        hidden_all, cot_all, contract_first, preferred_element_type=jnp.float32
    ).astype(jnp.bfloat16)
    grad_gate = lax.dot_general(
        tokens_all, dgate_all, contract_first, preferred_element_type=jnp.float32
    ).astype(jnp.bfloat16)
    grad_up = lax.dot_general(
        tokens_all, dup_all, contract_first, preferred_element_type=jnp.float32
    ).astype(jnp.bfloat16)
    def col_partial(rows):
        return tokens_major(
            jnp.concatenate(
                [
                    jnp.dot(
                        acts_all[rows, :hidden_cols], down_weight, preferred_element_type=jnp.float32
                    ).astype(jnp.bfloat16),
                    (
                        lax.dot_general(
                            acts_all[rows, hidden_cols : 2 * hidden_cols],
                            gate_weight,
                            contract_last,
                            preferred_element_type=jnp.float32,
                        )
                        + lax.dot_general(
                            acts_all[rows, 2 * hidden_cols :],
                            up_weight,
                            contract_last,
                            preferred_element_type=jnp.float32,
                        )
                    ).astype(jnp.bfloat16),
                ],
                axis=1,
            )
        )

    half = acts_all.shape[0] // 2
    sent = swap_cores(col_partial(slice(half, None)))
    chip_sums = col_partial(slice(0, half)).astype(jnp.float32) + sent.astype(jnp.float32)
    out_sums = sum_by_exchange(chip_sums.astype(jnp.bfloat16), CHIPS, lax.psum(1, CHIPS))
    output = out_sums[:, :feat_cols].astype(jnp.bfloat16)
    grad_masked = out_sums[:, feat_cols:]
    grad_frames = jnp.where(keep_mask, grad_masked, jnp.zeros_like(grad_masked)).astype(
        jnp.bfloat16
    )
    return (output, grad_frames, grad_gate, grad_up, grad_down)


def solution(mesh):
    n_row, n_col = mesh.devices.shape
    split = Mesh(mesh.devices.reshape(n_row, n_col // 4, 2, 2), ("row",) + COL)
    placed = (
        P(COL, "row"),
        P(COL, "row"),
        P("row", COL),
        P("row", COL),
        P(COL, "row"),
        P(),
        P(),
        P(),
        P(),
        P(),
        P(),
    )
    return jax.shard_map(
        shards,
        mesh=split,
        in_specs=placed,
        out_specs=(
            P(COL, "row"),
            P(COL, "row"),
            P("row", COL),
            P("row", COL),
            P(COL, "row"),
        ),
        check_vma=False,
    )
```

```python
import jax
import jax.numpy as jnp
from jax import lax
from jax.experimental.layout import Layout, with_layout_constraint
from jax.sharding import Mesh, PartitionSpec as P

COL = ("cz", "cx", "cc")
CHIPS = ("cz", "cx")
CORE = "cc"


def span_masks(
    utt_ids,
    tok_index,
    feat_index,
    valid_len,
    time_start,
    time_width,
    freq_start,
    freq_width,
):
    utt_index = jnp.arange(valid_len.shape[0], dtype=jnp.int32)
    starts = jnp.sum((utt_ids[None, :] < utt_index[:, None]).astype(jnp.int32), axis=1)
    ends = jnp.sum((utt_ids[None, :] <= utt_index[:, None]).astype(jnp.int32), axis=1)
    member = (
        (tok_index[:, None] >= starts[None, :]) & (tok_index[:, None] < ends[None, :])
    ).astype(jnp.int32)

    def lookup(table):
        return jnp.sum(member * table[None, :], axis=1)

    position = tok_index - lookup(starts)
    valid_rows = position < lookup(valid_len)
    time_low = lookup(time_start)
    in_time = (position >= time_low) & (position < time_low + lookup(time_width))
    freq_low = lookup(freq_start)[:, None]
    freq_high = freq_low + lookup(freq_width)[:, None]
    in_freq = (feat_index[None, :] >= freq_low) & (feat_index[None, :] < freq_high)
    keep_mask = (valid_rows & jnp.logical_not(in_time))[:, None] & jnp.logical_not(in_freq)
    return (keep_mask, valid_rows)


def tokens_major(value):
    return with_layout_constraint(value, Layout((0, 1)))


def swap_cores(value):
    return lax.ppermute(value, CORE, [(0, 1), (1, 0)])


def gather_by_exchange(part, axis, count):
    spread = jnp.broadcast_to(part[None], (count,) + part.shape)
    got = lax.all_to_all(spread, axis, 0, 0)
    return got.reshape((count * part.shape[0],) + part.shape[1:])


def sum_by_exchange(partial, axis, count):
    split = partial.reshape((count, partial.shape[0] // count) + partial.shape[1:])
    got = lax.all_to_all(split, axis, 0, 0)
    if count == 16:
        grouped = got.astype(jnp.float32).reshape((4, 4) + got.shape[1:])
        return jnp.sum(lax.optimization_barrier(jnp.sum(grouped, axis=1)), axis=0)
    if count > 2:
        return jnp.sum(got.astype(jnp.float32), axis=0)
    return got[0].astype(jnp.float32) + got[1].astype(jnp.float32)


def shards(
    frames,
    cotangent,
    gate_weight,
    up_weight,
    down_weight,
    utt_ids,
    valid_len,
    time_start,
    time_width,
    freq_start,
    freq_width,
):
    tok_rows, feat_cols = frames.shape
    hidden_cols = gate_weight.shape[1]
    first_tok = lax.axis_index(COL) * tok_rows
    first_feat = lax.axis_index("row") * feat_cols
    tok_index = first_tok + jnp.arange(tok_rows, dtype=jnp.int32)
    feat_index = first_feat + jnp.arange(feat_cols, dtype=jnp.int32)
    keep_mask, valid_rows = span_masks(
        utt_ids,
        tok_index,
        feat_index,
        valid_len,
        time_start,
        time_width,
        freq_start,
        freq_width,
    )
    masked = jnp.where(keep_mask, frames, jnp.zeros_like(frames))
    cot_valid = jnp.where(valid_rows[:, None], cotangent, jnp.zeros_like(cotangent))
    contract_last = (((1,), (1,)), ((), ()))
    contract_first = (((0,), (0,)), ((), ()))
    both = jnp.concatenate([masked, cot_valid], axis=1)
    both_own = gather_by_exchange(both, CHIPS, lax.psum(1, CHIPS))
    both_all = jnp.concatenate([both_own, swap_cores(both_own)], axis=0)
    tokens_all = both_all[:, :feat_cols]
    cot_all = both_all[:, feat_cols:]
    sums = sum_by_exchange(
        jnp.concatenate(
            [
                jnp.dot(tokens_all, gate_weight, preferred_element_type=jnp.float32),
                jnp.dot(tokens_all, up_weight, preferred_element_type=jnp.float32),
                lax.dot_general(
                    cot_all, down_weight, contract_last, preferred_element_type=jnp.float32
                ),
            ],
            axis=1,
        ).astype(jnp.bfloat16),
        "row",
        lax.psum(1, "row"),
    )
    gate = sums[:, :hidden_cols]
    up = sums[:, hidden_cols : 2 * hidden_cols]
    grad_hidden = sums[:, 2 * hidden_cols :]
    sigmoid_gate = jax.nn.sigmoid(gate)
    hidden = (gate * sigmoid_gate * up).astype(jnp.bfloat16)
    dgate = (grad_hidden * up * sigmoid_gate * (1.0 + gate * (1.0 - sigmoid_gate))).astype(
        jnp.bfloat16
    )
    dup = (grad_hidden * gate * sigmoid_gate).astype(jnp.bfloat16)
    acts_all = gather_by_exchange(
        jnp.concatenate([hidden, dgate, dup], axis=1), "row", lax.psum(1, "row")
    )
    hidden_all = acts_all[:, :hidden_cols]
    dgate_all = acts_all[:, hidden_cols : 2 * hidden_cols]
    dup_all = acts_all[:, 2 * hidden_cols :]
    grad_down = lax.dot_general(
        hidden_all, cot_all, contract_first, preferred_element_type=jnp.float32
    ).astype(jnp.bfloat16)
    grad_gate = lax.dot_general(
        tokens_all, dgate_all, contract_first, preferred_element_type=jnp.float32
    ).astype(jnp.bfloat16)
    grad_up = lax.dot_general(
        tokens_all, dup_all, contract_first, preferred_element_type=jnp.float32
    ).astype(jnp.bfloat16)
    out_partial = jnp.concatenate(
        [
            jnp.dot(hidden_all, down_weight, preferred_element_type=jnp.float32).astype(
                jnp.bfloat16
            ),
            (
                lax.dot_general(
                    dgate_all, gate_weight, contract_last, preferred_element_type=jnp.float32
                )
                + lax.dot_general(
                    dup_all, up_weight, contract_last, preferred_element_type=jnp.float32
                )
            ).astype(jnp.bfloat16),
        ],
        axis=1,
    )
    out_partial = tokens_major(out_partial)
    half = out_partial.shape[0] // 2
    chip_sums = out_partial[:half].astype(jnp.float32) + swap_cores(out_partial[half:]).astype(
        jnp.float32
    )
    out_sums = sum_by_exchange(chip_sums.astype(jnp.bfloat16), CHIPS, lax.psum(1, CHIPS))
    output = out_sums[:, :feat_cols].astype(jnp.bfloat16)
    grad_masked = out_sums[:, feat_cols:]
    grad_frames = jnp.where(keep_mask, grad_masked, jnp.zeros_like(grad_masked)).astype(
        jnp.bfloat16
    )
    return (output, grad_frames, grad_gate, grad_up, grad_down)


def solution(mesh):
    n_row, n_col = mesh.devices.shape
    split = Mesh(mesh.devices.reshape(n_row, n_col // 4, 2, 2), ("row",) + COL)
    placed = (
        P(COL, "row"),
        P(COL, "row"),
        P("row", COL),
        P("row", COL),
        P(COL, "row"),
        P(),
        P(),
        P(),
        P(),
        P(),
        P(),
    )
    return jax.shard_map(
        shards,
        mesh=split,
        in_specs=placed,
        out_specs=(
            P(COL, "row"),
            P(COL, "row"),
            P("row", COL),
            P("row", COL),
            P(COL, "row"),
        ),
        check_vma=False,
    )
```

```python
import jax
import jax.numpy as jnp
from jax import lax
from jax.experimental.layout import Layout, with_layout_constraint
from jax.sharding import Mesh, PartitionSpec as P

COL = ("cz", "cx", "cc")
CHIPS = ("cz", "cx")
CORE = "cc"


def span_masks(
    utt_ids,
    tok_index,
    feat_index,
    valid_len,
    time_start,
    time_width,
    freq_start,
    freq_width,
):
    utt_index = jnp.arange(valid_len.shape[0], dtype=jnp.int32)
    starts = jnp.sum((utt_ids[None, :] < utt_index[:, None]).astype(jnp.int32), axis=1)
    ends = jnp.sum((utt_ids[None, :] <= utt_index[:, None]).astype(jnp.int32), axis=1)
    member = (
        (tok_index[:, None] >= starts[None, :]) & (tok_index[:, None] < ends[None, :])
    ).astype(jnp.int32)

    def lookup(table):
        return jnp.sum(member * table[None, :], axis=1)

    position = tok_index - lookup(starts)
    valid_rows = position < lookup(valid_len)
    time_low = lookup(time_start)
    in_time = (position >= time_low) & (position < time_low + lookup(time_width))
    freq_low = lookup(freq_start)[:, None]
    freq_high = freq_low + lookup(freq_width)[:, None]
    in_freq = (feat_index[None, :] >= freq_low) & (feat_index[None, :] < freq_high)
    keep_mask = (valid_rows & jnp.logical_not(in_time))[:, None] & jnp.logical_not(in_freq)
    return (keep_mask, valid_rows)


def tokens_major(value):
    return with_layout_constraint(value, Layout((0, 1)))


def swap_cores(value):
    return lax.ppermute(value, CORE, [(0, 1), (1, 0)])


def gather_by_exchange(part, axis, count):
    spread = jnp.broadcast_to(part[None], (count,) + part.shape)
    got = lax.all_to_all(spread, axis, 0, 0)
    return got.reshape((count * part.shape[0],) + part.shape[1:])


def sum_by_exchange(partial, axis, count):
    split = partial.reshape((count, partial.shape[0] // count) + partial.shape[1:])
    got = lax.all_to_all(split, axis, 0, 0)
    if count > 2:
        return jnp.sum(got.astype(jnp.float32), axis=0)
    return got[0].astype(jnp.float32) + got[1].astype(jnp.float32)


def shards(
    frames,
    cotangent,
    gate_weight,
    up_weight,
    down_weight,
    utt_ids,
    valid_len,
    time_start,
    time_width,
    freq_start,
    freq_width,
):
    tok_rows, feat_cols = frames.shape
    hidden_cols = gate_weight.shape[1]
    first_tok = lax.axis_index(COL) * tok_rows
    first_feat = lax.axis_index("row") * feat_cols
    tok_index = first_tok + jnp.arange(tok_rows, dtype=jnp.int32)
    feat_index = first_feat + jnp.arange(feat_cols, dtype=jnp.int32)
    keep_mask, valid_rows = span_masks(
        utt_ids,
        tok_index,
        feat_index,
        valid_len,
        time_start,
        time_width,
        freq_start,
        freq_width,
    )
    masked = jnp.where(keep_mask, frames, jnp.zeros_like(frames))
    cot_valid = jnp.where(valid_rows[:, None], cotangent, jnp.zeros_like(cotangent))
    contract_last = (((1,), (1,)), ((), ()))
    contract_first = (((0,), (0,)), ((), ()))
    both = jnp.concatenate([masked, cot_valid], axis=1)
    both_own = gather_by_exchange(both, CHIPS, lax.psum(1, CHIPS))
    both_all = jnp.concatenate([both_own, swap_cores(both_own)], axis=0)
    tokens_all = both_all[:, :feat_cols]
    cot_all = both_all[:, feat_cols:]
    sums = sum_by_exchange(
        jnp.concatenate(
            [
                jnp.dot(tokens_all, gate_weight, preferred_element_type=jnp.float32),
                jnp.dot(tokens_all, up_weight, preferred_element_type=jnp.float32),
                lax.dot_general(
                    cot_all, down_weight, contract_last, preferred_element_type=jnp.float32
                ),
            ],
            axis=1,
        ).astype(jnp.bfloat16),
        "row",
        lax.psum(1, "row"),
    )
    gate = sums[:, :hidden_cols]
    up = sums[:, hidden_cols : 2 * hidden_cols]
    grad_hidden = sums[:, 2 * hidden_cols :]
    sigmoid_gate = jax.nn.sigmoid(gate)
    hidden = (gate * sigmoid_gate * up).astype(jnp.bfloat16)
    dgate = (grad_hidden * up * sigmoid_gate * (1.0 + gate * (1.0 - sigmoid_gate))).astype(
        jnp.bfloat16
    )
    dup = (grad_hidden * gate * sigmoid_gate).astype(jnp.bfloat16)
    acts_all = gather_by_exchange(
        jnp.concatenate([hidden, dgate, dup], axis=1), "row", lax.psum(1, "row")
    )
    hidden_all = acts_all[:, :hidden_cols]
    dgate_all = acts_all[:, hidden_cols : 2 * hidden_cols]
    dup_all = acts_all[:, 2 * hidden_cols :]
    grad_down = lax.dot_general(
        hidden_all, cot_all, contract_first, preferred_element_type=jnp.float32
    ).astype(jnp.bfloat16)
    grad_gate = lax.dot_general(
        tokens_all, dgate_all, contract_first, preferred_element_type=jnp.float32
    ).astype(jnp.bfloat16)
    grad_up = lax.dot_general(
        tokens_all, dup_all, contract_first, preferred_element_type=jnp.float32
    ).astype(jnp.bfloat16)
    def col_partial(rows):
        return tokens_major(
            jnp.concatenate(
                [
                    jnp.dot(
                        acts_all[rows, :hidden_cols], down_weight, preferred_element_type=jnp.float32
                    ).astype(jnp.bfloat16),
                    (
                        lax.dot_general(
                            acts_all[rows, hidden_cols : 2 * hidden_cols],
                            gate_weight,
                            contract_last,
                            preferred_element_type=jnp.float32,
                        )
                        + lax.dot_general(
                            acts_all[rows, 2 * hidden_cols :],
                            up_weight,
                            contract_last,
                            preferred_element_type=jnp.float32,
                        )
                    ).astype(jnp.bfloat16),
                ],
                axis=1,
            )
        )

    half = acts_all.shape[0] // 2
    sent = swap_cores(col_partial(slice(half, None)))
    chip_sums = col_partial(slice(0, half)).astype(jnp.float32) + sent.astype(jnp.float32)
    out_sums = sum_by_exchange(chip_sums.astype(jnp.bfloat16), CHIPS, lax.psum(1, CHIPS))
    output = out_sums[:, :feat_cols].astype(jnp.bfloat16)
    grad_masked = out_sums[:, feat_cols:]
    grad_frames = jnp.where(keep_mask, grad_masked, jnp.zeros_like(grad_masked)).astype(
        jnp.bfloat16
    )
    return (output, grad_frames, grad_gate, grad_up, grad_down)


def solution(mesh):
    n_row, n_col = mesh.devices.shape
    split = Mesh(mesh.devices.reshape(n_row, n_col // 4, 2, 2), ("row",) + COL)
    placed = (
        P(COL, "row"),
        P(COL, "row"),
        P("row", COL),
        P("row", COL),
        P(COL, "row"),
        P(),
        P(),
        P(),
        P(),
        P(),
        P(),
    )
    return jax.shard_map(
        shards,
        mesh=split,
        in_specs=placed,
        out_specs=(
            P(COL, "row"),
            P(COL, "row"),
            P("row", COL),
            P("row", COL),
            P(COL, "row"),
        ),
        check_vma=False,
    )
```
